32 devices in a mesh: gx: 4 (over y, x), gy: 4 (over z), gz: 2 (over core).
Axes of the slice: x: 2, y: 2, z: 4, core: 2. Of those that a mesh axis runs over, the one named last changes fastest.
Arguments:
- concentration: bfloat16 [256, 128, 256], P(('gx', 'gy'), None, 'gz'), may hold values from 0.00016 to 10.5
- turbulence: bfloat16 [256, 128, 256], P(('gx', 'gy'), None, 'gz'), may hold values from 0.049804688 to 2
- src_list: int32 [256, 4], P(('gx', 'gy')), may hold values from 0 to 255, as said below
- interp_weights: bfloat16 [256, 4, 128, 128], P(('gx', 'gy')), may hold values from 0 to 0.5
- settle_class: int32 [256, 8], P(('gx', 'gy'), 'gz'), may hold values from 0 to 7
- kappa_table: float32 [2, 8], replicated, may hold values from 3 to 30000
- fall_table: float32 [8], replicated, may hold values from 1 to 4
Outputs:
- concentration_out: bfloat16 [256, 128, 256], P(('gx', 'gy'), None, 'gz')
- turbulence_out: bfloat16 [256, 128, 256], P(('gx', 'gy'), None, 'gz')
- mass_ratio: float32 [2], replicated
The draws below stay inside these ranges and needn't reach their ends.
Inputs may be any that keep to these rules, and one draw needn't show every extreme that they name: `src_list`: every entry names a tile held by a device with the same gx index as the entry's own tile. Of the 64 entries of one device, exactly 8 name tiles of other devices; at most 4 of them name tiles of any one device, and on every device exactly 4 name tiles of some one device.
All inputs are finite; a program needn't handle non-finite values.
Results may differ from the reference program's by a relative error of at most 0.0026.
Values may be sent and summed in bfloat16 or wider, within the bound.
No kernel may reach another device: no remote copies, remote signals or barrier semaphores. Data moves between devices by JAX's collectives and lax.ppermute only.
A program may use at most 64 MiB of HBM per device.

```python
import math
import jax
import jax.numpy as jnp
from jax import lax

COLS = 128
TPD = 16
KSRC = 4
ZB = 32
NCLS = 8
STEPS = 2
REMOTE = 8
CAP = 4
TILES = 256
NZ = 256
N_GX = 4
N_GY = 4


def surge_phase(key):
    return jax.random.randint(jax.random.fold_in(key, 99991), (), 0, 2)


def surge_rows(key):
    tile_row = jnp.arange(TILES, dtype=jnp.int32) // (TPD * N_GY)
    return (tile_row + surge_phase(key)) % 2 == 0


def draw_concentration(key, part):
    key_cell, key_tile, key_decay = jax.random.split(jax.random.fold_in(key, 17), 3)
    tile_position = jnp.arange(TILES, dtype=jnp.float32) / max(TILES - 1, 1)
    surging = surge_rows(key)
    rising = 1.0 + 2.0 * tile_position
    cell_factor = jax.random.uniform(key_cell, (TILES, COLS, NZ), jnp.float32, 0.5, 1.5)
    tile_scale = jnp.exp(jax.random.uniform(key_tile, (TILES,), jnp.float32, 0.0, 2.302585))
    decay_depth = jnp.exp(jax.random.uniform(key_decay, (TILES,), jnp.float32, 0.693147, 1.791759))
    level_index = jnp.arange(NZ, dtype=jnp.float32)
    height = jnp.where(surging[:, None], level_index[None, :], NZ - 1.0 - level_index[None, :])
    profile = 0.01 + 0.99 * jnp.exp(-height / decay_depth[:, None])
    sampled = 0.2 * (rising * tile_scale)[:, None, None] * profile[:, None, :] * cell_factor
    return sampled.astype(jnp.bfloat16)


def draw_interp_weights(key, part):
    key_gain, key_shift, key_side = jax.random.split(jax.random.fold_in(key, 23), 3)
    surging = surge_rows(key)
    row_share = jnp.where(surging, 1.4, 0.3).astype(jnp.float32)
    diagonal_gain = jax.random.uniform(key_gain, (TILES, KSRC, COLS), jnp.float32, 0.6, 1.4)
    side_ratio = jax.random.uniform(key_side, (TILES, KSRC, COLS), jnp.float32, 0.25, 0.6)
    shift_code = jax.random.randint(key_shift, (TILES, KSRC, COLS), 0, 6)
    offset = shift_code - 3 + (shift_code >= 3).astype(jnp.int32)
    column_index = jnp.arange(COLS, dtype=jnp.int32)
    target = (column_index[None, None, :] + offset) % COLS
    identity = (column_index[:, None] == column_index[None, :]).astype(jnp.float32)
    beside = (target[..., None] == column_index).astype(jnp.float32)
    sampled = row_share[:, None, None, None] * diagonal_gain[..., None] * (identity + side_ratio[..., None] * beside) / KSRC
    return sampled.astype(jnp.bfloat16)


def draw_src_list(key, part):
    devices = N_GX * N_GY
    entry_count = TPD * KSRC

    def per_device(device_index):
        device_key = jax.random.fold_in(key, device_index)
        key_order, key_peer, key_spare, key_local = jax.random.split(device_key, 4)
        row_index = device_index // N_GY
        lane_index = device_index % N_GY
        entry_order = jax.random.permutation(key_order, entry_count)
        peer_order = jax.random.permutation(key_peer, N_GY - 1)
        spare_slots = jax.random.permutation(key_spare, (N_GY - 2) * CAP) + CAP
        chosen = jnp.concatenate([jnp.arange(CAP, dtype=jnp.int32), spare_slots[:REMOTE - CAP].astype(jnp.int32)])
        peer_lane = peer_order[chosen // CAP].astype(jnp.int32)
        peer_lane = peer_lane + (peer_lane >= lane_index).astype(jnp.int32)
        owner_lane = jnp.full((entry_count,), lane_index, jnp.int32).at[entry_order[:REMOTE]].set(peer_lane)
        local_tile = jax.random.randint(key_local, (entry_count,), 0, TPD)
        global_ids = (row_index * N_GY + owner_lane) * TPD + local_tile
        return global_ids.astype(jnp.int32).reshape(TPD, KSRC)
    return jax.vmap(per_device)(jnp.arange(devices, dtype=jnp.int32)).reshape(devices * TPD, KSRC)


def plant(entries, stream_key, least, largest):
    place = [jax.random.randint(jax.random.fold_in(stream_key, axis), (), 0, length) for axis, length in enumerate(entries.shape)]
    longest = entries.shape.index(max(entries.shape))
    beside = place[:longest] + [(place[longest] + 1) % entries.shape[longest]] + place[longest + 1:]
    return entries.at[tuple(place)].set(least).at[tuple(beside)].set(largest)


def levels(rng, dims, cuts, least, high):
    loudness = 1.0
    for position, parts in cuts:
        draws = jax.random.uniform(jax.random.fold_in(jax.random.fold_in(rng, 6), position), (parts,), jnp.float32, least / len(cuts), high / len(cuts))
        loudness = loudness * jnp.repeat(jnp.exp(draws), dims[position] // parts).reshape((-1,) + (1,) * (len(dims) - 1 - position))
    return loudness


def setup_inputs(seed: int = 0) -> dict:
    streams_of = jax.random.split(jax.random.key(seed), 8)
    return {
        "concentration": draw_concentration(jax.random.fold_in(streams_of[7], 71), 0),
        "turbulence": jnp.clip(jnp.exp(math.log(2.0) - 3.6927934 * jax.random.uniform(streams_of[1], (TILES, COLS, NZ), jnp.float32) ** levels(streams_of[1], (TILES, COLS, NZ), ((0, 16), (2, 2)), -0.2, 0.2)), 0.049804688, 2.0).astype(jnp.bfloat16),
        "src_list": draw_src_list(jax.random.fold_in(streams_of[7], 71), 0),
        "interp_weights": draw_interp_weights(jax.random.fold_in(streams_of[7], 71), 0),
        "settle_class": plant(jax.random.randint(streams_of[4], (TILES, NZ // ZB), 0, NCLS), jax.random.fold_in(streams_of[4], 1), 0, NCLS - 1).astype(jnp.int32),
        "kappa_table": jnp.clip(jnp.exp(jax.random.uniform(streams_of[5], (2, NCLS), jnp.float32, math.log(3.0), math.log(30000.0))), 3.0, 30000.0),
        "fall_table": jnp.clip(jnp.exp(jax.random.uniform(streams_of[6], (NCLS,), jnp.float32, math.log(1.0), math.log(4.0))), 1.0, 4.0),
    }


HIGHEST = lax.Precision.HIGHEST

def coefficients(settle_class, kappa_row, fall_row):
    level_class = jnp.repeat(settle_class, ZB, axis=1)
    onehot = (level_class[..., None] == jnp.arange(NCLS, dtype=jnp.int32)).astype(jnp.float32)
    diffusion = jnp.einsum('tzq,q->tz', onehot, kappa_row, precision=HIGHEST)
    falling = jnp.einsum('tzq,q->tz', onehot, fall_row, precision=HIGHEST)
    level_index = jnp.arange(NZ, dtype=jnp.int32)
    diffusion = jnp.where(level_index[None, :] >= 1, diffusion, jnp.zeros_like(diffusion))
    boundary = jnp.zeros((diffusion.shape[0], 1), diffusion.dtype)
    diffusion_up = jnp.concatenate([diffusion[:, 1:], boundary], axis=1)
    fall_up = jnp.concatenate([falling[:, 1:], boundary], axis=1)
    return (-diffusion, 1.0 + diffusion + diffusion_up + falling, -(diffusion_up + fall_up))

def reference(concentration, turbulence, src_list, interp_weights, settle_class, kappa_table, fall_table):
    blocks = TILES // TPD
    systems = [coefficients(settle_class, kappa_table[0], fall_table), coefficients(settle_class, kappa_table[1], jnp.zeros_like(fall_table))]
    systems = [tuple((member.reshape(blocks, TPD, NZ) for member in system)) for system in systems]
    source_blocks = src_list.reshape(blocks, TPD, KSRC)
    weight_blocks = interp_weights.reshape(blocks, TPD, KSRC, COLS, COLS)
    fields = jnp.stack([concentration, turbulence], axis=1)
    ratios = []
    for step_index in range(STEPS):

        def advect(packed, current=fields):
            sources, weights = packed
            summed = jnp.zeros((TPD, 2, COLS, NZ), jnp.float32)
            for entry_k in range(KSRC):
                picked = current[sources[:, entry_k]].astype(jnp.float32)
                summed = summed + jnp.einsum('tcd,tfdz->tfcz', weights[:, entry_k].astype(jnp.float32), picked, precision=HIGHEST)
            return summed
        advected = lax.map(advect, (source_blocks, weight_blocks))
        mass_fixer = jnp.sum(fields[:, 0].astype(jnp.float32)) / jnp.sum(advected[:, :, 0])
        ratios.append(mass_fixer)
        scaling = jnp.stack([mass_fixer, jnp.ones_like(mass_fixer)])
        advected = advected * scaling[None, None, :, None, None]

        def settle(packed):
            advected_block, first_system, second_system = packed
            solved = []
            for field_id, system in enumerate((first_system, second_system)):
                right_side = jnp.swapaxes(advected_block[:, field_id], 1, 2)
                answer = lax.linalg.tridiagonal_solve(system[0], system[1], system[2], right_side)
                solved.append(jnp.swapaxes(answer, 1, 2))
            return jnp.stack(solved, axis=1).astype(jnp.bfloat16)
        fields = lax.map(settle, (advected, systems[0], systems[1])).reshape(TILES, 2, COLS, NZ)
    return (fields[:, 0], fields[:, 1], jnp.stack(ratios))
```

```python
import jax
import jax.numpy as jnp
from jax import lax
from jax.sharding import PartitionSpec as P
from jax.experimental import pallas as pl
from jax.experimental.pallas import tpu as pltpu

STEPS = 2


HIGHEST = lax.Precision.HIGHEST


def passed_along(array, axis, by):
    devices = lax.axis_size(axis)
    pairs = [(i, i + by) for i in range(devices) if 0 <= i + by < devices]
    return lax.ppermute(array, axis, pairs)


def from_partner(array, axis, apart):
    return lax.ppermute(array, axis, [(i, i ^ 1 << apart) for i in range(lax.axis_size(axis))])


def bucket_ranks(owners, wanted, buckets):
    onehot = (
        (owners[..., None] == jnp.arange(buckets, dtype=jnp.int32)) & wanted[..., None]
    ).astype(jnp.int32)
    running = jnp.cumsum(onehot, axis=-2) - 1
    return jnp.sum(onehot * running, axis=-1)


def table_lookup(level_class, lookup_table):
    classes = lookup_table.shape[-1]
    onehot = (level_class[..., None] == jnp.arange(classes, dtype=jnp.int32)).astype(jnp.float32)
    return jnp.einsum("tzq,fq->tfz", onehot, lookup_table, precision=HIGHEST)


def thomas_inverse_kernel(lower_ref, diagonal_ref, upper_ref, inverse_ref, ratio_ref):
    levels = inverse_ref.shape[0]
    lane = lax.broadcasted_iota(jnp.int32, inverse_ref.shape[1:], 1)
    pivot = 1.0 / diagonal_ref[0]
    ratio = upper_ref[0] * pivot
    row = jnp.where(lane == 0, 1.0, 0.0) * pivot
    ratio_ref[0] = ratio
    inverse_ref[0] = row

    def forward(z, carry):
        ratio, row = carry
        below = lower_ref[z]
        pivot = 1.0 / (diagonal_ref[z] - below * ratio)
        ratio = upper_ref[z] * pivot
        row = (jnp.where(lane == z, 1.0, 0.0) - below * row) * pivot
        ratio_ref[z] = ratio
        inverse_ref[z] = row
        return ratio, row

    _, row = lax.fori_loop(1, levels, forward, (ratio, row))

    def backward(step, row):
        z = levels - 2 - step
        row = inverse_ref[z] - ratio_ref[z] * row
        inverse_ref[z] = row
        return row

    lax.fori_loop(0, levels - 1, backward, row)


def block_inverse(lower, diagonal, upper):
    lead = diagonal.shape[:-1]
    levels = diagonal.shape[-1]
    systems = diagonal.size // levels

    def level_major(band):
        return jnp.transpose(band.reshape(systems, levels))[:, :, None]

    inverse = pl.pallas_call(
        thomas_inverse_kernel,
        out_shape=jax.ShapeDtypeStruct((levels, systems, levels), jnp.float32),
        scratch_shapes=[pltpu.VMEM((levels, systems, 1), jnp.float32)],
    )(level_major(lower), level_major(diagonal), level_major(upper))
    return jnp.transpose(inverse, (1, 0, 2)).reshape(lead + (levels, levels))


def interface_values(low_value, low_spike, high_value, high_spike):
    lower_end = (low_value - low_spike[..., None] * high_value) / (1.0 - low_spike * high_spike)[
        ..., None
    ]
    upper_end = high_value - high_spike[..., None] * lower_end
    return (lower_end, upper_end)


def per_device(
    concentration, turbulence, src_list, interp_weights, settle_class, kappa_table, fall_table
):
    tiles_here, columns, levels = concentration.shape
    sources_per = src_list.shape[1]
    lane_count = lax.axis_size("gy")
    my_lane = lax.axis_index("gy")
    layers = lax.axis_size("gz")
    my_layer = lax.axis_index("gz")
    remote_count = tiles_here // 2
    capacity = max(2, 3 * remote_count // (2 * (lane_count - 1)))
    entries = src_list.reshape(-1)
    owner_lane = entries // tiles_here % lane_count
    local_tile = entries % tiles_here
    remote = owner_lane != my_lane
    slot_index = bucket_ranks(owner_lane, remote, lane_count)
    requests = (
        jnp.zeros((lane_count, capacity), jnp.int32)
        .at[jnp.where(remote, owner_lane, lane_count), slot_index]
        .set(local_tile, mode="drop")
    )
    pool_index = jnp.where(
        remote, tiles_here + owner_lane * capacity + slot_index, local_tile
    ).reshape(tiles_here, sources_per)
    level_class = jnp.repeat(settle_class, levels // settle_class.shape[1], axis=1)
    both_fall = jnp.stack([fall_table, jnp.zeros_like(fall_table)])
    diffusion = table_lookup(level_class, kappa_table)
    falling = table_lookup(level_class, both_fall)
    global_level = my_layer * levels + jnp.arange(levels, dtype=jnp.int32)
    diffusion = jnp.where(global_level >= 1, diffusion, 0.0)
    above_class = passed_along(settle_class[:, :1], "gz", -1)
    at_top = my_layer == layers - 1
    diffusion_above = jnp.where(at_top, 0.0, table_lookup(above_class, kappa_table))
    fall_above = jnp.where(at_top, 0.0, table_lookup(above_class, both_fall))
    diffusion_up = jnp.concatenate([diffusion[..., 1:], diffusion_above], axis=-1)
    fall_up = jnp.concatenate([falling[..., 1:], fall_above], axis=-1)
    diagonal = 1.0 + diffusion + diffusion_up + falling
    lower_band = -diffusion
    upper_band = -(diffusion_up + fall_up)
    level_index = jnp.arange(levels, dtype=jnp.int32)
    block_lower = jnp.where(level_index == 0, 0.0, lower_band)
    block_upper = jnp.where(level_index == levels - 1, 0.0, upper_band)
    inverse = block_inverse(block_lower, diagonal, block_upper)
    spike_column = jnp.where(
        my_layer == 0,
        upper_band[..., -1:] * inverse[..., :, levels - 1],
        lower_band[..., :1] * inverse[..., :, 0],
    )
    edge_spike = jnp.where(my_layer == 0, spike_column[..., -1], spike_column[..., 0])
    fields = jnp.stack([concentration, turbulence], axis=1)
    field_ids = jnp.arange(2, dtype=jnp.int32)[None, :, None]
    ratios = []
    for step_index in range(STEPS):
        arrived = lax.all_to_all(
            fields[lax.all_to_all(requests, "gy", split_axis=0, concat_axis=0, tiled=True)],
            "gy",
            split_axis=0,
            concat_axis=0,
            tiled=True,
        )
        tile_pool = jnp.concatenate([fields, arrived.reshape((-1,) + fields.shape[1:])], axis=0)
        advected = jnp.zeros(fields.shape, jnp.float32)
        for entry_k in range(sources_per):
            advected = advected + jnp.einsum(
                "tcd,tfdz->tfcz",
                interp_weights[:, entry_k],
                tile_pool[pool_index[:, entry_k]],
                preferred_element_type=jnp.float32,
            )
        totals = lax.psum(
            (jnp.sum(fields[:, 0], dtype=jnp.float32), jnp.sum(advected[:, 0])), ("gx", "gy", "gz")
        )
        mass_fixer = totals[0] / totals[1]
        ratios.append(mass_fixer)
        advected = advected * jnp.where(field_ids == 0, mass_fixer, 1.0)[..., None]
        solved = jnp.einsum(
            "tfzy,tfcy->tfcz",
            inverse,
            advected,
            precision=HIGHEST,
            preferred_element_type=jnp.float32,
        )
        edge_value = jnp.where(my_layer == 0, solved[..., -1], solved[..., 0])
        partner_field = 1 - my_layer
        send_value = lax.dynamic_index_in_dim(edge_value, partner_field, 1, keepdims=False)
        send_spike = lax.dynamic_index_in_dim(edge_spike, partner_field, 1, keepdims=False)
        other_value, other_spike = from_partner((send_value, send_spike), "gz", 0)
        own_value = lax.dynamic_index_in_dim(edge_value, my_layer, 1, keepdims=False)
        own_spike = lax.dynamic_index_in_dim(edge_spike, my_layer, 1, keepdims=False)
        low_value = jnp.where(my_layer == 0, own_value, other_value)
        low_spike = jnp.where(my_layer == 0, own_spike, other_spike)
        high_value = jnp.where(my_layer == 0, other_value, own_value)
        high_spike = jnp.where(my_layer == 0, other_spike, own_spike)
        lower_end, upper_end = interface_values(low_value, low_spike, high_value, high_spike)
        keeping = jnp.where(my_layer == 0, upper_end, lower_end)
        giving = jnp.where(my_layer == 0, lower_end, upper_end)
        received = from_partner(giving, "gz", 0)
        needed = jnp.where(field_ids == my_layer, keeping[:, None, :], received[:, None, :])
        fields = (solved - spike_column[:, :, None, :] * needed[..., None]).astype(jnp.bfloat16)
    return (fields[:, 0], fields[:, 1], jnp.stack(ratios))


def solution(mesh):
    return jax.shard_map(
        per_device,
        mesh=mesh,
        in_specs=(
            P(("gx", "gy"), None, "gz"),
            P(("gx", "gy"), None, "gz"),
            P(("gx", "gy"), None),
            P(("gx", "gy"), None, None, None),
            P(("gx", "gy"), "gz"),
            P(),
            P(),
        ),
        out_specs=(P(("gx", "gy"), None, "gz"), P(("gx", "gy"), None, "gz"), P()),
        check_vma=False,
    )
```

```python
import jax
import jax.numpy as jnp
from jax import lax
from jax.sharding import PartitionSpec as P
from jax.experimental import pallas as pl
from jax.experimental.pallas import tpu as pltpu

STEPS = 2


HIGHEST = lax.Precision.HIGHEST


def passed_along(array, axis, by):
    devices = lax.axis_size(axis)
    pairs = [(i, i + by) for i in range(devices) if 0 <= i + by < devices]
    return lax.ppermute(array, axis, pairs)


def from_partner(array, axis, apart):
    return lax.ppermute(array, axis, [(i, i ^ 1 << apart) for i in range(lax.axis_size(axis))])


def butterfly_sum(value, axes):
    for axis in axes:
        devices = lax.axis_size(axis)
        if devices & (devices - 1):
            value = lax.psum(value, axis)
            continue
        bit = 1
        while bit < devices:
            value = value + lax.ppermute(value, axis, [(i, i ^ bit) for i in range(devices)])
            bit *= 2
    return value


def bucket_ranks(owners, wanted, buckets):
    onehot = (
        (owners[..., None] == jnp.arange(buckets, dtype=jnp.int32)) & wanted[..., None]
    ).astype(jnp.int32)
    running = jnp.cumsum(onehot, axis=-2) - 1
    return jnp.sum(onehot * running, axis=-1)


def table_lookup(level_class, lookup_table):
    classes = lookup_table.shape[-1]
    onehot = (level_class[..., None] == jnp.arange(classes, dtype=jnp.int32)).astype(jnp.float32)
    return jnp.einsum("tzq,fq->tfz", onehot, lookup_table, precision=HIGHEST)


def thomas_inverse_kernel(lower_ref, diagonal_ref, upper_ref, inverse_ref, ratio_ref):
    levels = inverse_ref.shape[0]
    lane = lax.broadcasted_iota(jnp.int32, inverse_ref.shape[1:], 1)
    pivot = 1.0 / diagonal_ref[0]
    ratio = upper_ref[0] * pivot
    row = jnp.where(lane == 0, 1.0, 0.0) * pivot
    ratio_ref[0] = ratio
    inverse_ref[0] = row

    def forward(z, carry):
        ratio, row = carry
        below = lower_ref[z]
        pivot = 1.0 / (diagonal_ref[z] - below * ratio)
        ratio = upper_ref[z] * pivot
        row = (jnp.where(lane == z, 1.0, 0.0) - below * row) * pivot
        ratio_ref[z] = ratio
        inverse_ref[z] = row
        return ratio, row

    _, row = lax.fori_loop(1, levels, forward, (ratio, row))

    def backward(step, row):
        z = levels - 2 - step
        row = inverse_ref[z] - ratio_ref[z] * row
        inverse_ref[z] = row
        return row

    lax.fori_loop(0, levels - 1, backward, row)


def block_inverse(lower, diagonal, upper):
    lead = diagonal.shape[:-1]
    levels = diagonal.shape[-1]
    systems = diagonal.size // levels

    def level_major(band):
        return jnp.transpose(band.reshape(systems, levels))[:, :, None]

    inverse = pl.pallas_call(
        thomas_inverse_kernel,
        out_shape=jax.ShapeDtypeStruct((levels, systems, levels), jnp.float32),
        scratch_shapes=[pltpu.VMEM((levels, systems, 1), jnp.float32)],
    )(level_major(lower), level_major(diagonal), level_major(upper))
    return jnp.transpose(inverse, (1, 0, 2)).reshape(lead + (levels, levels))


def interface_values(low_value, low_spike, high_value, high_spike):
    lower_end = (low_value - low_spike[..., None] * high_value) / (1.0 - low_spike * high_spike)[
        ..., None
    ]
    upper_end = high_value - high_spike[..., None] * lower_end
    return (lower_end, upper_end)


def per_device(
    concentration, turbulence, src_list, interp_weights, settle_class, kappa_table, fall_table
):
    tiles_here, columns, levels = concentration.shape
    sources_per = src_list.shape[1]
    lane_count = lax.axis_size("gy")
    my_lane = lax.axis_index("gy")
    layers = lax.axis_size("gz")
    my_layer = lax.axis_index("gz")
    remote_count = tiles_here // 2
    capacity = max(2, 3 * remote_count // (2 * (lane_count - 1)))
    entries = src_list.reshape(-1)
    owner_lane = entries // tiles_here % lane_count
    local_tile = entries % tiles_here
    remote = owner_lane != my_lane
    slot_index = bucket_ranks(owner_lane, remote, lane_count)
    match = (
        remote[None, None, :]
        & (owner_lane[None, None, :] == jnp.arange(lane_count, dtype=jnp.int32)[:, None, None])
        & (slot_index[None, None, :] == jnp.arange(capacity, dtype=jnp.int32)[None, :, None])
    )
    requests = jnp.sum(jnp.where(match, local_tile[None, None, :], 0), axis=-1, dtype=jnp.int32)
    pool_index = jnp.where(
        remote, tiles_here + owner_lane * capacity + slot_index, local_tile
    ).reshape(tiles_here, sources_per)
    level_class = jnp.repeat(settle_class, levels // settle_class.shape[1], axis=1)
    both_fall = jnp.stack([fall_table, jnp.zeros_like(fall_table)])
    diffusion = table_lookup(level_class, kappa_table)
    falling = table_lookup(level_class, both_fall)
    global_level = my_layer * levels + jnp.arange(levels, dtype=jnp.int32)
    diffusion = jnp.where(global_level >= 1, diffusion, 0.0)
    above_class = passed_along(settle_class[:, :1], "gz", -1)
    at_top = my_layer == layers - 1
    diffusion_above = jnp.where(at_top, 0.0, table_lookup(above_class, kappa_table))
    fall_above = jnp.where(at_top, 0.0, table_lookup(above_class, both_fall))
    diffusion_up = jnp.concatenate([diffusion[..., 1:], diffusion_above], axis=-1)
    fall_up = jnp.concatenate([falling[..., 1:], fall_above], axis=-1)
    diagonal = 1.0 + diffusion + diffusion_up + falling
    lower_band = -diffusion
    upper_band = -(diffusion_up + fall_up)
    level_index = jnp.arange(levels, dtype=jnp.int32)
    block_lower = jnp.where(level_index == 0, 0.0, lower_band)
    block_upper = jnp.where(level_index == levels - 1, 0.0, upper_band)
    inverse = block_inverse(block_lower, diagonal, block_upper)
    spike_column = jnp.where(
        my_layer == 0,
        upper_band[..., -1:] * inverse[..., :, levels - 1],
        lower_band[..., :1] * inverse[..., :, 0],
    )
    edge_spike = jnp.where(my_layer == 0, spike_column[..., -1], spike_column[..., 0])
    fields = jnp.stack([concentration, turbulence], axis=1)
    field_ids = jnp.arange(2, dtype=jnp.int32)[None, :, None]
    ratios = []
    for step_index in range(STEPS):
        arrived = lax.all_to_all(
            fields[lax.all_to_all(requests, "gy", split_axis=0, concat_axis=0, tiled=True)],
            "gy",
            split_axis=0,
            concat_axis=0,
            tiled=True,
        )
        tile_pool = jnp.concatenate([fields, arrived.reshape((-1,) + fields.shape[1:])], axis=0)
        advected = jnp.zeros(fields.shape, jnp.float32)
        for entry_k in range(sources_per):
            advected = advected + jnp.einsum(
                "tcd,tfdz->tfcz",
                interp_weights[:, entry_k],
                tile_pool[pool_index[:, entry_k]],
                preferred_element_type=jnp.float32,
            )
        totals = butterfly_sum(
            jnp.stack([jnp.sum(fields[:, 0], dtype=jnp.float32), jnp.sum(advected[:, 0])]),
            ("gz", "gy", "gx"),
        )
        mass_fixer = totals[0] / totals[1]
        ratios.append(mass_fixer)
        advected = advected * jnp.where(field_ids == 0, mass_fixer, 1.0)[..., None]
        solved = jnp.einsum(
            "tfzy,tfcy->tfcz",
            inverse,
            advected,
            precision=HIGHEST,
            preferred_element_type=jnp.float32,
        )
        edge_value = jnp.where(my_layer == 0, solved[..., -1], solved[..., 0])
        partner_field = 1 - my_layer
        send_value = lax.dynamic_index_in_dim(edge_value, partner_field, 1, keepdims=False)
        send_spike = lax.dynamic_index_in_dim(edge_spike, partner_field, 1, keepdims=False)
        other_value, other_spike = from_partner((send_value, send_spike), "gz", 0)
        own_value = lax.dynamic_index_in_dim(edge_value, my_layer, 1, keepdims=False)
        own_spike = lax.dynamic_index_in_dim(edge_spike, my_layer, 1, keepdims=False)
        low_value = jnp.where(my_layer == 0, own_value, other_value)
        low_spike = jnp.where(my_layer == 0, own_spike, other_spike)
        high_value = jnp.where(my_layer == 0, other_value, own_value)
        high_spike = jnp.where(my_layer == 0, other_spike, own_spike)
        lower_end, upper_end = interface_values(low_value, low_spike, high_value, high_spike)
        keeping = jnp.where(my_layer == 0, upper_end, lower_end)
        giving = jnp.where(my_layer == 0, lower_end, upper_end)
        received = from_partner(giving, "gz", 0)
        needed = jnp.where(field_ids == my_layer, keeping[:, None, :], received[:, None, :])
        fields = (solved - spike_column[:, :, None, :] * needed[..., None]).astype(jnp.bfloat16)
    return (fields[:, 0], fields[:, 1], jnp.stack(ratios))


def solution(mesh):
    return jax.shard_map(
        per_device,
        mesh=mesh,
        in_specs=(
            P(("gx", "gy"), None, "gz"),
            P(("gx", "gy"), None, "gz"),
            P(("gx", "gy"), None),
            P(("gx", "gy"), None, None, None),
            P(("gx", "gy"), "gz"),
            P(),
            P(),
        ),
        out_specs=(P(("gx", "gy"), None, "gz"), P(("gx", "gy"), None, "gz"), P()),
        check_vma=False,
    )
```

```python
import jax
import jax.numpy as jnp
from jax import lax
from jax.sharding import PartitionSpec as P
from jax.experimental import pallas as pl
from jax.experimental.pallas import tpu as pltpu

STEPS = 2


HIGHEST = lax.Precision.HIGHEST


def passed_along(array, axis, by):
    devices = lax.axis_size(axis)
    pairs = [(i, i + by) for i in range(devices) if 0 <= i + by < devices]
    return lax.ppermute(array, axis, pairs)


def from_partner(array, axis, apart):
    return lax.ppermute(array, axis, [(i, i ^ 1 << apart) for i in range(lax.axis_size(axis))])


def butterfly_sum(value, axes):
    for axis in axes:
        devices = lax.axis_size(axis)
        if devices & (devices - 1):
            value = lax.psum(value, axis)
            continue
        bit = 1
        while bit < devices:
            value = value + lax.ppermute(value, axis, [(i, i ^ bit) for i in range(devices)])
            bit *= 2
    return value


def bucket_ranks(owners, wanted, buckets):
    onehot = (
        (owners[..., None] == jnp.arange(buckets, dtype=jnp.int32)) & wanted[..., None]
    ).astype(jnp.int32)
    running = jnp.cumsum(onehot, axis=-2) - 1
    return jnp.sum(onehot * running, axis=-1)


def table_lookup(level_class, lookup_table):
    classes = lookup_table.shape[-1]
    onehot = (level_class[..., None] == jnp.arange(classes, dtype=jnp.int32)).astype(jnp.float32)
    return jnp.einsum("tzq,fq->tfz", onehot, lookup_table, precision=HIGHEST)


def thomas_inverse_kernel(lower_ref, diagonal_ref, upper_ref, inverse_ref, ratio_ref):
    levels = inverse_ref.shape[0]
    lane = lax.broadcasted_iota(jnp.int32, inverse_ref.shape[1:], 1)
    pivot = 1.0 / diagonal_ref[0]
    ratio = upper_ref[0] * pivot
    row = jnp.where(lane == 0, 1.0, 0.0) * pivot
    ratio_ref[0] = ratio
    inverse_ref[0] = row

    def forward(z, carry):
        ratio, row = carry
        below = lower_ref[z]
        pivot = 1.0 / (diagonal_ref[z] - below * ratio)
        ratio = upper_ref[z] * pivot
        row = (jnp.where(lane == z, 1.0, 0.0) - below * row) * pivot
        ratio_ref[z] = ratio
        inverse_ref[z] = row
        return ratio, row

    _, row = lax.fori_loop(1, levels, forward, (ratio, row))

    def backward(step, row):
        z = levels - 2 - step
        row = inverse_ref[z] - ratio_ref[z] * row
        inverse_ref[z] = row
        return row

    lax.fori_loop(0, levels - 1, backward, row)


def block_inverse(lower, diagonal, upper):
    lead = diagonal.shape[:-1]
    levels = diagonal.shape[-1]
    systems = diagonal.size // levels

    def level_major(band):
        return jnp.transpose(band.reshape(systems, levels))[:, :, None]

    inverse = pl.pallas_call(
        thomas_inverse_kernel,
        out_shape=jax.ShapeDtypeStruct((levels, systems, levels), jnp.float32),
        scratch_shapes=[pltpu.VMEM((levels, systems, 1), jnp.float32)],
    )(level_major(lower), level_major(diagonal), level_major(upper))
    return jnp.transpose(inverse, (1, 0, 2)).reshape(lead + (levels, levels))


def interface_values(low_value, low_spike, high_value, high_spike):
    lower_end = (low_value - low_spike[..., None] * high_value) / (1.0 - low_spike * high_spike)[
        ..., None
    ]
    upper_end = high_value - high_spike[..., None] * lower_end
    return (lower_end, upper_end)


def per_device(
    concentration, turbulence, src_list, interp_weights, settle_class, kappa_table, fall_table
):
    tiles_here, columns, levels = concentration.shape
    sources_per = src_list.shape[1]
    lane_count = lax.axis_size("gy")
    my_lane = lax.axis_index("gy")
    layers = lax.axis_size("gz")
    my_layer = lax.axis_index("gz")
    remote_count = tiles_here // 2
    capacity = max(2, 3 * remote_count // (2 * (lane_count - 1)))
    entries = src_list.reshape(-1)
    owner_lane = entries // tiles_here % lane_count
    local_tile = entries % tiles_here
    remote = owner_lane != my_lane
    slot_index = bucket_ranks(owner_lane, remote, lane_count)
    match = (
        remote[None, None, :]
        & (owner_lane[None, None, :] == jnp.arange(lane_count, dtype=jnp.int32)[:, None, None])
        & (slot_index[None, None, :] == jnp.arange(capacity, dtype=jnp.int32)[None, :, None])
    )
    requests = jnp.sum(jnp.where(match, local_tile[None, None, :], 0), axis=-1, dtype=jnp.int32)
    shift = (my_lane - owner_lane) % lane_count
    pool_index = jnp.where(
        remote, tiles_here + (shift - 1) * capacity + slot_index, local_tile
    ).reshape(tiles_here, sources_per)
    level_class = jnp.repeat(settle_class, levels // settle_class.shape[1], axis=1)
    both_fall = jnp.stack([fall_table, jnp.zeros_like(fall_table)])
    diffusion = table_lookup(level_class, kappa_table)
    falling = table_lookup(level_class, both_fall)
    global_level = my_layer * levels + jnp.arange(levels, dtype=jnp.int32)
    diffusion = jnp.where(global_level >= 1, diffusion, 0.0)
    above_class = passed_along(settle_class[:, :1], "gz", -1)
    at_top = my_layer == layers - 1
    diffusion_above = jnp.where(at_top, 0.0, table_lookup(above_class, kappa_table))
    fall_above = jnp.where(at_top, 0.0, table_lookup(above_class, both_fall))
    diffusion_up = jnp.concatenate([diffusion[..., 1:], diffusion_above], axis=-1)
    fall_up = jnp.concatenate([falling[..., 1:], fall_above], axis=-1)
    diagonal = 1.0 + diffusion + diffusion_up + falling
    lower_band = -diffusion
    upper_band = -(diffusion_up + fall_up)
    level_index = jnp.arange(levels, dtype=jnp.int32)
    block_lower = jnp.where(level_index == 0, 0.0, lower_band)
    block_upper = jnp.where(level_index == levels - 1, 0.0, upper_band)
    inverse = block_inverse(block_lower, diagonal, block_upper)
    spike_column = jnp.where(
        my_layer == 0,
        upper_band[..., -1:] * inverse[..., :, levels - 1],
        lower_band[..., :1] * inverse[..., :, 0],
    )
    edge_spike = jnp.where(my_layer == 0, spike_column[..., -1], spike_column[..., 0])
    other_spike = from_partner(edge_spike, "gz", 0)
    low_spike = jnp.where(my_layer == 0, edge_spike, other_spike)
    high_spike = jnp.where(my_layer == 0, other_spike, edge_spike)
    fields = jnp.stack([concentration, turbulence], axis=1)
    wanted = lax.all_to_all(requests, "gy", split_axis=0, concat_axis=0, tiled=True)

    def exchange(tiles):
        received = []
        for hop in range(1, lane_count):
            target = (my_lane + hop) % lane_count
            block = tiles[lax.dynamic_index_in_dim(wanted, target, 0, keepdims=False)]
            received.append(
                lax.ppermute(block, "gy", [(i, (i + hop) % lane_count) for i in range(lane_count)])
            )
        return jnp.concatenate(received, axis=0)

    arrived = exchange(fields)
    ratios = []
    for step_index in range(STEPS):
        tile_pool = jnp.concatenate([fields, arrived], axis=0)
        advected = jnp.zeros(fields.shape, jnp.float32)
        for entry_k in range(sources_per):
            advected = advected + jnp.einsum(
                "tcd,tfdz->tfcz",
                interp_weights[:, entry_k],
                tile_pool[pool_index[:, entry_k]],
                preferred_element_type=jnp.float32,
            )
        totals = butterfly_sum(
            jnp.stack([jnp.sum(fields[:, 0], dtype=jnp.float32), jnp.sum(advected[:, 0])]),
            ("gz", "gy", "gx"),
        )
        solved = jnp.einsum(
            "tfzy,tfcy->tfcz",
            inverse,
            advected,
            precision=HIGHEST,
            preferred_element_type=jnp.float32,
        )
        edge_value = jnp.where(my_layer == 0, solved[..., -1], solved[..., 0])
        other_value = from_partner(edge_value, "gz", 0)
        low_value = jnp.where(my_layer == 0, edge_value, other_value)
        high_value = jnp.where(my_layer == 0, other_value, edge_value)
        lower_end, upper_end = interface_values(low_value, low_spike, high_value, high_spike)
        needed = jnp.where(my_layer == 0, upper_end, lower_end)
        unscaled = solved - spike_column[:, :, None, :] * needed[..., None]
        mass_fixer = totals[0] / totals[1]
        ratios.append(mass_fixer)
        next_turbulence = unscaled[:, 1].astype(jnp.bfloat16)
        if step_index + 1 < STEPS:
            sent = exchange(
                jnp.stack([unscaled[:, 0], next_turbulence.astype(jnp.float32)], axis=1)
            )
            arrived = jnp.stack(
                [(mass_fixer * sent[:, 0]).astype(jnp.bfloat16), sent[:, 1].astype(jnp.bfloat16)],
                axis=1,
            )
        fields = jnp.stack(
            [(mass_fixer * unscaled[:, 0]).astype(jnp.bfloat16), next_turbulence], axis=1
        )
    return (fields[:, 0], fields[:, 1], jnp.stack(ratios))


def solution(mesh):
    return jax.shard_map(
        per_device,
        mesh=mesh,
        in_specs=(
            P(("gx", "gy"), None, "gz"),
            P(("gx", "gy"), None, "gz"),
            P(("gx", "gy"), None),
            P(("gx", "gy"), None, None, None),
            P(("gx", "gy"), "gz"),
            P(),
            P(),
        ),
        out_specs=(P(("gx", "gy"), None, "gz"), P(("gx", "gy"), None, "gz"), P()),
        check_vma=False,
    )
```

```python
import jax
import jax.numpy as jnp
from jax import lax
from jax.sharding import PartitionSpec as P
from jax.experimental import pallas as pl
from jax.experimental.pallas import tpu as pltpu

STEPS = 2


HIGHEST = lax.Precision.HIGHEST


def passed_along(array, axis, by):
    devices = lax.axis_size(axis)
    pairs = [(i, i + by) for i in range(devices) if 0 <= i + by < devices]
    return lax.ppermute(array, axis, pairs)


def from_partner(array, axis, apart):
    return lax.ppermute(array, axis, [(i, i ^ 1 << apart) for i in range(lax.axis_size(axis))])


def butterfly_sum(value, axes):
    for axis in axes:
        devices = lax.axis_size(axis)
        if devices & (devices - 1):
            value = lax.psum(value, axis)
            continue
        bit = 1
        while bit < devices:
            value = value + lax.ppermute(value, axis, [(i, i ^ bit) for i in range(devices)])
            bit *= 2
    return value


def bucket_ranks(owners, wanted, buckets):
    onehot = (
        (owners[..., None] == jnp.arange(buckets, dtype=jnp.int32)) & wanted[..., None]
    ).astype(jnp.int32)
    running = jnp.cumsum(onehot, axis=-2) - 1
    return jnp.sum(onehot * running, axis=-1)


def table_lookup(level_class, lookup_table):
    classes = lookup_table.shape[-1]
    onehot = (level_class[..., None] == jnp.arange(classes, dtype=jnp.int32)).astype(jnp.float32)
    return jnp.einsum("tzq,fq->tfz", onehot, lookup_table, precision=HIGHEST)


def thomas_inverse_kernel(lower_ref, diagonal_ref, upper_ref, inverse_ref, ratio_ref):
    levels = inverse_ref.shape[0]
    lane = lax.broadcasted_iota(jnp.int32, inverse_ref.shape[1:], 1)
    pivot = 1.0 / diagonal_ref[0]
    ratio = upper_ref[0] * pivot
    row = jnp.where(lane == 0, 1.0, 0.0) * pivot
    ratio_ref[0] = ratio
    inverse_ref[0] = row

    def forward(z, carry):
        ratio, row = carry
        below = lower_ref[z]
        pivot = 1.0 / (diagonal_ref[z] - below * ratio)
        ratio = upper_ref[z] * pivot
        row = (jnp.where(lane == z, 1.0, 0.0) - below * row) * pivot
        ratio_ref[z] = ratio
        inverse_ref[z] = row
        return ratio, row

    _, row = lax.fori_loop(1, levels, forward, (ratio, row), unroll=8)

    def backward(step, row):
        z = levels - 2 - step
        row = inverse_ref[z] - ratio_ref[z] * row
        inverse_ref[z] = row
        return row

    lax.fori_loop(0, levels - 1, backward, row, unroll=8)


def block_inverse(lower, diagonal, upper, ready):
    lead = diagonal.shape[:-1]
    levels = diagonal.shape[-1]
    systems = diagonal.size // levels

    def level_major(band):
        return jnp.transpose(band.reshape(systems, levels))[:, :, None]

    bands, ready = lax.optimization_barrier(
        ((level_major(lower), level_major(diagonal), level_major(upper)), ready)
    )
    inverse = pl.pallas_call(
        thomas_inverse_kernel,
        out_shape=jax.ShapeDtypeStruct((levels, systems, levels), jnp.float32),
        scratch_shapes=[pltpu.VMEM((levels, systems, 1), jnp.float32)],
        cost_estimate=pl.CostEstimate(
            flops=16 * levels * systems * levels,
            transcendentals=levels * systems,
            bytes_accessed=64 * levels * systems * levels,
        ),
    )(*bands)
    return jnp.transpose(inverse, (1, 0, 2)).reshape(lead + (levels, levels)), ready


def interface_values(low_value, low_spike, high_value, high_spike):
    lower_end = (low_value - low_spike[..., None] * high_value) / (1.0 - low_spike * high_spike)[
        ..., None
    ]
    upper_end = high_value - high_spike[..., None] * lower_end
    return (lower_end, upper_end)


def per_device(
    concentration, turbulence, src_list, interp_weights, settle_class, kappa_table, fall_table
):
    tiles_here, columns, levels = concentration.shape
    sources_per = src_list.shape[1]
    lane_count = lax.axis_size("gy")
    my_lane = lax.axis_index("gy")
    layers = lax.axis_size("gz")
    my_layer = lax.axis_index("gz")
    remote_count = tiles_here // 2
    capacity = max(2, 3 * remote_count // (2 * (lane_count - 1)))
    entries = src_list.reshape(-1)
    owner_lane = entries // tiles_here % lane_count
    local_tile = entries % tiles_here
    remote = owner_lane != my_lane
    slot_index = bucket_ranks(owner_lane, remote, lane_count)
    match = (
        remote[None, None, :]
        & (owner_lane[None, None, :] == jnp.arange(lane_count, dtype=jnp.int32)[:, None, None])
        & (slot_index[None, None, :] == jnp.arange(capacity, dtype=jnp.int32)[None, :, None])
    )
    requests = jnp.sum(jnp.where(match, local_tile[None, None, :], 0), axis=-1, dtype=jnp.int32)
    shift = (my_lane - owner_lane) % lane_count
    pool_index = jnp.where(
        remote, tiles_here + (shift - 1) * capacity + slot_index, local_tile
    ).reshape(tiles_here, sources_per)
    level_class = jnp.repeat(settle_class, levels // settle_class.shape[1], axis=1)
    both_fall = jnp.stack([fall_table, jnp.zeros_like(fall_table)])
    diffusion = table_lookup(level_class, kappa_table)
    falling = table_lookup(level_class, both_fall)
    global_level = my_layer * levels + jnp.arange(levels, dtype=jnp.int32)
    diffusion = jnp.where(global_level >= 1, diffusion, 0.0)
    above_class = passed_along(settle_class[:, :1], "gz", -1)
    at_top = my_layer == layers - 1
    diffusion_above = jnp.where(at_top, 0.0, table_lookup(above_class, kappa_table))
    fall_above = jnp.where(at_top, 0.0, table_lookup(above_class, both_fall))
    diffusion_up = jnp.concatenate([diffusion[..., 1:], diffusion_above], axis=-1)
    fall_up = jnp.concatenate([falling[..., 1:], fall_above], axis=-1)
    diagonal = 1.0 + diffusion + diffusion_up + falling
    lower_band = -diffusion
    upper_band = -(diffusion_up + fall_up)
    level_index = jnp.arange(levels, dtype=jnp.int32)
    block_lower = jnp.where(level_index == 0, 0.0, lower_band)
    block_upper = jnp.where(level_index == levels - 1, 0.0, upper_band)
    fields = jnp.stack([concentration, turbulence], axis=1)
    wanted = lax.all_to_all(requests, "gy", split_axis=0, concat_axis=0, tiled=True)

    def exchange(tiles, extra=None):
        received = []
        for hop in range(1, lane_count):
            target = (my_lane + hop) % lane_count
            block = tiles[lax.dynamic_index_in_dim(wanted, target, 0, keepdims=False)]
            if extra is not None:
                block = jnp.concatenate([block.reshape(-1), extra])
            received.append(
                lax.ppermute(block, "gy", [(i, (i + hop) % lane_count) for i in range(lane_count)])
            )
        if extra is None:
            return jnp.concatenate(received, axis=0), None
        tail = extra.shape[0]
        shape = (-1,) + tiles.shape[1:]
        tiles_in = jnp.concatenate([r[:-tail].reshape(shape) for r in received], axis=0)
        extras_in = jnp.stack([extra] + [r[-tail:] for r in received])
        by_lane = extras_in[(my_lane - jnp.arange(lane_count)) % lane_count]
        total = by_lane[0]
        for lane in range(1, lane_count):
            total = total + by_lane[lane]
        return tiles_in, total

    arrived, _ = exchange(fields)
    inverse, wanted = block_inverse(block_lower, diagonal, block_upper, wanted)
    spike_column = jnp.where(
        my_layer == 0,
        upper_band[..., -1:] * inverse[..., :, levels - 1],
        lower_band[..., :1] * inverse[..., :, 0],
    )
    edge_spike = jnp.where(my_layer == 0, spike_column[..., -1], spike_column[..., 0])
    other_spike = from_partner(edge_spike, "gz", 0)
    low_spike = jnp.where(my_layer == 0, edge_spike, other_spike)
    high_spike = jnp.where(my_layer == 0, other_spike, edge_spike)
    ratios = []
    for step_index in range(STEPS):
        tile_pool = jnp.concatenate([fields, arrived], axis=0)
        advected = jnp.zeros(fields.shape, jnp.float32)
        for entry_k in range(sources_per):
            advected = advected + jnp.einsum(
                "tcd,tfdz->tfcz",
                interp_weights[:, entry_k],
                tile_pool[pool_index[:, entry_k]],
                preferred_element_type=jnp.float32,
            )
        partial = jnp.stack([jnp.sum(fields[:, 0], dtype=jnp.float32), jnp.sum(advected[:, 0])])
        last = step_index + 1 == STEPS
        if last:
            totals = butterfly_sum(partial, ("gz", "gy", "gx"))
        else:
            partial = butterfly_sum(partial, ("gz", "gx"))
        solved = jnp.einsum(
            "tfzy,tfcy->tfcz",
            inverse,
            advected,
            precision=HIGHEST,
            preferred_element_type=jnp.float32,
        )
        edge_value = jnp.where(my_layer == 0, solved[..., -1], solved[..., 0])
        other_value = from_partner(edge_value, "gz", 0)
        low_value = jnp.where(my_layer == 0, edge_value, other_value)
        high_value = jnp.where(my_layer == 0, other_value, edge_value)
        lower_end, upper_end = interface_values(low_value, low_spike, high_value, high_spike)
        needed = jnp.where(my_layer == 0, upper_end, lower_end)
        unscaled = solved - spike_column[:, :, None, :] * needed[..., None]
        next_turbulence = unscaled[:, 1].astype(jnp.bfloat16)
        if not last:
            sent, totals = exchange(
                jnp.stack([unscaled[:, 0], next_turbulence.astype(jnp.float32)], axis=1), partial
            )
        mass_fixer = totals[0] / totals[1]
        ratios.append(mass_fixer)
        if not last:
            arrived = jnp.stack(
                [(mass_fixer * sent[:, 0]).astype(jnp.bfloat16), sent[:, 1].astype(jnp.bfloat16)],
                axis=1,
            )
        fields = jnp.stack(
            [(mass_fixer * unscaled[:, 0]).astype(jnp.bfloat16), next_turbulence], axis=1
        )
    return (fields[:, 0], fields[:, 1], jnp.stack(ratios))


def solution(mesh):
    return jax.shard_map(
        per_device,
        mesh=mesh,
        in_specs=(
            P(("gx", "gy"), None, "gz"),
            P(("gx", "gy"), None, "gz"),
            P(("gx", "gy"), None),
            P(("gx", "gy"), None, None, None),
            P(("gx", "gy"), "gz"),
            P(),
            P(),
        ),
        out_specs=(P(("gx", "gy"), None, "gz"), P(("gx", "gy"), None, "gz"), P()),
        check_vma=False,
    )
```

```python
import jax
import jax.numpy as jnp
from jax import lax
from jax.sharding import PartitionSpec as P
from jax.experimental import pallas as pl
from jax.experimental.pallas import tpu as pltpu

STEPS = 2


HIGHEST = lax.Precision.HIGHEST


def passed_along(array, axis, by):
    devices = lax.axis_size(axis)
    pairs = [(i, i + by) for i in range(devices) if 0 <= i + by < devices]
    return lax.ppermute(array, axis, pairs)


def from_partner(array, axis, apart):
    return lax.ppermute(array, axis, [(i, i ^ 1 << apart) for i in range(lax.axis_size(axis))])


def butterfly_sum(value, axes):
    for axis in axes:
        devices = lax.axis_size(axis)
        if devices & (devices - 1):
            value = lax.psum(value, axis)
            continue
        bit = 1
        while bit < devices:
            value = value + lax.ppermute(value, axis, [(i, i ^ bit) for i in range(devices)])
            bit *= 2
    return value


def bucket_ranks(owners, wanted, buckets):
    onehot = (
        (owners[..., None] == jnp.arange(buckets, dtype=jnp.int32)) & wanted[..., None]
    ).astype(jnp.int32)
    running = jnp.cumsum(onehot, axis=-2) - 1
    return jnp.sum(onehot * running, axis=-1)


def table_lookup(level_class, lookup_table):
    classes = lookup_table.shape[-1]
    onehot = (level_class[..., None] == jnp.arange(classes, dtype=jnp.int32)).astype(jnp.float32)
    return jnp.einsum("tzq,fq->tfz", onehot, lookup_table, precision=HIGHEST)


def thomas_inverse_kernel(lower_ref, diagonal_ref, upper_ref, inverse_ref, ratio_ref):
    levels = inverse_ref.shape[0]
    lane = lax.broadcasted_iota(jnp.int32, inverse_ref.shape[1:], 1)
    pivot = 1.0 / diagonal_ref[0]
    ratio = upper_ref[0] * pivot
    row = jnp.where(lane == 0, 1.0, 0.0) * pivot
    ratio_ref[0] = ratio
    inverse_ref[0] = row

    def forward(z, carry):
        ratio, row = carry
        below = lower_ref[z]
        pivot = 1.0 / (diagonal_ref[z] - below * ratio)
        ratio = upper_ref[z] * pivot
        row = (jnp.where(lane == z, 1.0, 0.0) - below * row) * pivot
        ratio_ref[z] = ratio
        inverse_ref[z] = row
        return ratio, row

    _, row = lax.fori_loop(1, levels, forward, (ratio, row), unroll=8)

    def backward(step, row):
        z = levels - 2 - step
        row = inverse_ref[z] - ratio_ref[z] * row
        inverse_ref[z] = row
        return row

    lax.fori_loop(0, levels - 1, backward, row, unroll=8)


def block_inverse(lower, diagonal, upper, ready):
    lead = diagonal.shape[:-1]
    levels = diagonal.shape[-1]
    systems = diagonal.size // levels

    def level_major(band):
        return jnp.transpose(band.reshape(systems, levels))[:, :, None]

    bands, ready = lax.optimization_barrier(
        ((level_major(lower), level_major(diagonal), level_major(upper)), ready)
    )
    inverse = pl.pallas_call(
        thomas_inverse_kernel,
        out_shape=jax.ShapeDtypeStruct((levels, systems, levels), jnp.float32),
        scratch_shapes=[pltpu.VMEM((levels, systems, 1), jnp.float32)],
        cost_estimate=pl.CostEstimate(
            flops=16 * levels * systems * levels,
            transcendentals=levels * systems,
            bytes_accessed=64 * levels * systems * levels,
        ),
    )(*bands)
    return jnp.transpose(inverse, (1, 0, 2)).reshape(lead + (levels, levels)), ready


def advect_kernel(index_ref, weight_ref, *refs):
    tile_refs, out_ref = refs[:-1], refs[-1]
    for field in range(out_ref.shape[1]):
        total = None
        for entry_k, tile_ref in enumerate(tile_refs):
            term = jnp.dot(
                weight_ref[0, entry_k], tile_ref[0, field], preferred_element_type=jnp.float32
            )
            total = term if total is None else total + term
        out_ref[0, field] = total


def advect(weights, tile_pool, pool_index):
    tiles, sources = pool_index.shape
    _, fields, columns, levels = tile_pool.shape
    flat_index = pool_index.reshape(-1)

    def source_spec(entry_k):
        return pl.BlockSpec(
            (1, fields, columns, levels),
            lambda t, index, k=entry_k: (index[t * sources + k], 0, 0, 0),
        )

    return pl.pallas_call(
        advect_kernel,
        out_shape=jax.ShapeDtypeStruct((tiles, fields, columns, levels), jnp.float32),
        grid_spec=pltpu.PrefetchScalarGridSpec(
            num_scalar_prefetch=1,
            grid=(tiles,),
            in_specs=[pl.BlockSpec((1, sources, columns, columns), lambda t, index: (t, 0, 0, 0))]
            + [source_spec(k) for k in range(sources)],
            out_specs=pl.BlockSpec((1, fields, columns, levels), lambda t, index: (t, 0, 0, 0)),
        ),
        cost_estimate=pl.CostEstimate(
            flops=2 * tiles * sources * fields * columns * columns * levels,
            transcendentals=0,
            bytes_accessed=tiles * sources * (columns * columns + fields * columns * levels) * 2
            + tiles * fields * columns * levels * 4,
        ),
    )(flat_index, weights, *([tile_pool] * sources))


def interface_values(low_value, low_spike, high_value, high_spike):
    lower_end = (low_value - low_spike[..., None] * high_value) / (1.0 - low_spike * high_spike)[
        ..., None
    ]
    upper_end = high_value - high_spike[..., None] * lower_end
    return (lower_end, upper_end)


def per_device(
    concentration, turbulence, src_list, interp_weights, settle_class, kappa_table, fall_table
):
    tiles_here, columns, levels = concentration.shape
    sources_per = src_list.shape[1]
    lane_count = lax.axis_size("gy")
    my_lane = lax.axis_index("gy")
    layers = lax.axis_size("gz")
    my_layer = lax.axis_index("gz")
    remote_count = tiles_here // 2
    capacity = max(2, 3 * remote_count // (2 * (lane_count - 1)))
    entries = src_list.reshape(-1)
    owner_lane = entries // tiles_here % lane_count
    local_tile = entries % tiles_here
    remote = owner_lane != my_lane
    slot_index = bucket_ranks(owner_lane, remote, lane_count)
    match = (
        remote[None, None, :]
        & (owner_lane[None, None, :] == jnp.arange(lane_count, dtype=jnp.int32)[:, None, None])
        & (slot_index[None, None, :] == jnp.arange(capacity, dtype=jnp.int32)[None, :, None])
    )
    requests = jnp.sum(jnp.where(match, local_tile[None, None, :], 0), axis=-1, dtype=jnp.int32)
    shift = (my_lane - owner_lane) % lane_count
    pool_index = jnp.where(
        remote, tiles_here + (shift - 1) * capacity + slot_index, local_tile
    ).reshape(tiles_here, sources_per)
    level_class = jnp.repeat(settle_class, levels // settle_class.shape[1], axis=1)
    both_fall = jnp.stack([fall_table, jnp.zeros_like(fall_table)])
    diffusion = table_lookup(level_class, kappa_table)
    falling = table_lookup(level_class, both_fall)
    global_level = my_layer * levels + jnp.arange(levels, dtype=jnp.int32)
    diffusion = jnp.where(global_level >= 1, diffusion, 0.0)
    above_class = passed_along(settle_class[:, :1], "gz", -1)
    at_top = my_layer == layers - 1
    diffusion_above = jnp.where(at_top, 0.0, table_lookup(above_class, kappa_table))
    fall_above = jnp.where(at_top, 0.0, table_lookup(above_class, both_fall))
    diffusion_up = jnp.concatenate([diffusion[..., 1:], diffusion_above], axis=-1)
    fall_up = jnp.concatenate([falling[..., 1:], fall_above], axis=-1)
    diagonal = 1.0 + diffusion + diffusion_up + falling
    lower_band = -diffusion
    upper_band = -(diffusion_up + fall_up)
    level_index = jnp.arange(levels, dtype=jnp.int32)
    block_lower = jnp.where(level_index == 0, 0.0, lower_band)
    block_upper = jnp.where(level_index == levels - 1, 0.0, upper_band)
    fields = jnp.stack([concentration, turbulence], axis=1)
    wanted = lax.all_to_all(requests, "gy", split_axis=0, concat_axis=0, tiled=True)

    def exchange(tiles, extra=None):
        received = []
        for hop in range(1, lane_count):
            target = (my_lane + hop) % lane_count
            block = tiles[lax.dynamic_index_in_dim(wanted, target, 0, keepdims=False)]
            if extra is not None:
                block = jnp.concatenate([block.reshape(-1), extra])
            received.append(
                lax.ppermute(block, "gy", [(i, (i + hop) % lane_count) for i in range(lane_count)])
            )
        if extra is None:
            return jnp.concatenate(received, axis=0), None
        tail = extra.shape[0]
        shape = (-1,) + tiles.shape[1:]
        tiles_in = jnp.concatenate([r[:-tail].reshape(shape) for r in received], axis=0)
        extras_in = jnp.stack([extra] + [r[-tail:] for r in received])
        by_lane = extras_in[(my_lane - jnp.arange(lane_count)) % lane_count]
        total = by_lane[0]
        for lane in range(1, lane_count):
            total = total + by_lane[lane]
        return tiles_in, total

    arrived, _ = exchange(fields)
    inverse, wanted = block_inverse(block_lower, diagonal, block_upper, wanted)
    spike_column = jnp.where(
        my_layer == 0,
        upper_band[..., -1:] * inverse[..., :, levels - 1],
        lower_band[..., :1] * inverse[..., :, 0],
    )
    edge_spike = jnp.where(my_layer == 0, spike_column[..., -1], spike_column[..., 0])
    other_spike = from_partner(edge_spike, "gz", 0)
    low_spike = jnp.where(my_layer == 0, edge_spike, other_spike)
    high_spike = jnp.where(my_layer == 0, other_spike, edge_spike)
    ratios = []
    for step_index in range(STEPS):
        tile_pool = jnp.concatenate([fields, arrived], axis=0)
        advected = advect(interp_weights, tile_pool, pool_index)
        partial = jnp.stack([jnp.sum(fields[:, 0], dtype=jnp.float32), jnp.sum(advected[:, 0])])
        last = step_index + 1 == STEPS
        if last:
            totals = butterfly_sum(partial, ("gz", "gy", "gx"))
        else:
            partial = butterfly_sum(partial, ("gz", "gx"))
        solved = jnp.einsum(
            "tfzy,tfcy->tfcz",
            inverse,
            advected,
            precision=HIGHEST,
            preferred_element_type=jnp.float32,
        )
        edge_value = jnp.where(my_layer == 0, solved[..., -1], solved[..., 0])
        other_value = from_partner(edge_value, "gz", 0)
        low_value = jnp.where(my_layer == 0, edge_value, other_value)
        high_value = jnp.where(my_layer == 0, other_value, edge_value)
        lower_end, upper_end = interface_values(low_value, low_spike, high_value, high_spike)
        needed = jnp.where(my_layer == 0, upper_end, lower_end)
        unscaled = solved - spike_column[:, :, None, :] * needed[..., None]
        next_turbulence = unscaled[:, 1].astype(jnp.bfloat16)
        if not last:
            sent, totals = exchange(
                jnp.stack([unscaled[:, 0], next_turbulence.astype(jnp.float32)], axis=1), partial
            )
        mass_fixer = totals[0] / totals[1]
        ratios.append(mass_fixer)
        if not last:
            arrived = jnp.stack(
                [(mass_fixer * sent[:, 0]).astype(jnp.bfloat16), sent[:, 1].astype(jnp.bfloat16)],
                axis=1,
            )
        fields = jnp.stack(
            [(mass_fixer * unscaled[:, 0]).astype(jnp.bfloat16), next_turbulence], axis=1
        )
    return (fields[:, 0], fields[:, 1], jnp.stack(ratios))


def solution(mesh):
    return jax.shard_map(
        per_device,
        mesh=mesh,
        in_specs=(
            P(("gx", "gy"), None, "gz"),
            P(("gx", "gy"), None, "gz"),
            P(("gx", "gy"), None),
            P(("gx", "gy"), None, None, None),
            P(("gx", "gy"), "gz"),
            P(),
            P(),
        ),
        out_specs=(P(("gx", "gy"), None, "gz"), P(("gx", "gy"), None, "gz"), P()),
        check_vma=False,
    )
```

```python
import jax
import jax.numpy as jnp
from jax import lax
from jax.sharding import PartitionSpec as P
from jax.experimental import pallas as pl
from jax.experimental.pallas import tpu as pltpu

STEPS = 2


HIGHEST = lax.Precision.HIGHEST


def passed_along(array, axis, by):
    devices = lax.axis_size(axis)
    pairs = [(i, i + by) for i in range(devices) if 0 <= i + by < devices]
    return lax.ppermute(array, axis, pairs)


def from_partner(array, axis, apart):
    return lax.ppermute(array, axis, [(i, i ^ 1 << apart) for i in range(lax.axis_size(axis))])


def butterfly_sum(value, axes):
    for axis in axes:
        devices = lax.axis_size(axis)
        if devices & (devices - 1):
            value = lax.psum(value, axis)
            continue
        bit = 1
        while bit < devices:
            value = value + lax.ppermute(value, axis, [(i, i ^ bit) for i in range(devices)])
            bit *= 2
    return value


def bucket_ranks(owners, wanted, buckets):
    onehot = (
        (owners[..., None] == jnp.arange(buckets, dtype=jnp.int32)) & wanted[..., None]
    ).astype(jnp.int32)
    running = jnp.cumsum(onehot, axis=-2) - 1
    return jnp.sum(onehot * running, axis=-1)


def table_lookup(level_class, lookup_table):
    classes = lookup_table.shape[-1]
    onehot = (level_class[..., None] == jnp.arange(classes, dtype=jnp.int32)).astype(jnp.float32)
    return jnp.einsum("tzq,fq->tfz", onehot, lookup_table, precision=HIGHEST)


def thomas_inverse_kernel(lower_ref, diagonal_ref, upper_ref, inverse_ref, ratio_ref):
    levels = inverse_ref.shape[0]
    lane = lax.broadcasted_iota(jnp.int32, inverse_ref.shape[1:], 1)
    pivot = 1.0 / diagonal_ref[0]
    ratio = upper_ref[0] * pivot
    row = jnp.where(lane == 0, 1.0, 0.0) * pivot
    ratio_ref[0] = ratio
    inverse_ref[0] = row

    def forward(z, carry):
        ratio, row = carry
        below = lower_ref[z]
        pivot = 1.0 / (diagonal_ref[z] - below * ratio)
        ratio = upper_ref[z] * pivot
        row = (jnp.where(lane == z, 1.0, 0.0) - below * row) * pivot
        ratio_ref[z] = ratio
        inverse_ref[z] = row
        return ratio, row

    _, row = lax.fori_loop(1, levels, forward, (ratio, row), unroll=8)

    def backward(step, row):
        z = levels - 2 - step
        row = inverse_ref[z] - ratio_ref[z] * row
        inverse_ref[z] = row
        return row

    lax.fori_loop(0, levels - 1, backward, row, unroll=8)


def block_inverse(lower, diagonal, upper, ready):
    lead = diagonal.shape[:-1]
    levels = diagonal.shape[-1]
    systems = diagonal.size // levels

    def level_major(band):
        return jnp.transpose(band.reshape(systems, levels))[:, :, None]

    bands, ready = lax.optimization_barrier(
        ((level_major(lower), level_major(diagonal), level_major(upper)), ready)
    )
    inverse = pl.pallas_call(
        thomas_inverse_kernel,
        out_shape=jax.ShapeDtypeStruct((levels, systems, levels), jnp.float32),
        scratch_shapes=[pltpu.VMEM((levels, systems, 1), jnp.float32)],
        cost_estimate=pl.CostEstimate(
            flops=16 * levels * systems * levels,
            transcendentals=levels * systems,
            bytes_accessed=64 * levels * systems * levels,
        ),
    )(*bands)
    return jnp.transpose(inverse, (1, 0, 2)).reshape(lead + (levels, levels)), ready


def interface_values(low_value, low_spike, high_value, high_spike):
    lower_end = (low_value - low_spike[..., None] * high_value) / (1.0 - low_spike * high_spike)[
        ..., None
    ]
    upper_end = high_value - high_spike[..., None] * lower_end
    return (lower_end, upper_end)


def per_device(
    concentration, turbulence, src_list, interp_weights, settle_class, kappa_table, fall_table
):
    tiles_here, columns, levels = concentration.shape
    sources_per = src_list.shape[1]
    lane_count = lax.axis_size("gy")
    my_lane = lax.axis_index("gy")
    layers = lax.axis_size("gz")
    my_layer = lax.axis_index("gz")
    remote_count = tiles_here // 2
    capacity = max(2, 3 * remote_count // (2 * (lane_count - 1)))
    entries = src_list.reshape(-1)
    owner_lane = entries // tiles_here % lane_count
    local_tile = entries % tiles_here
    remote = owner_lane != my_lane
    slot_index = bucket_ranks(owner_lane, remote, lane_count)
    match = (
        remote[None, None, :]
        & (owner_lane[None, None, :] == jnp.arange(lane_count, dtype=jnp.int32)[:, None, None])
        & (slot_index[None, None, :] == jnp.arange(capacity, dtype=jnp.int32)[None, :, None])
    )
    requests = jnp.sum(jnp.where(match, local_tile[None, None, :], 0), axis=-1, dtype=jnp.int32)
    pool_index = jnp.where(
        remote, tiles_here + owner_lane * capacity + slot_index, local_tile
    ).reshape(tiles_here, sources_per)
    level_class = jnp.repeat(settle_class, levels // settle_class.shape[1], axis=1)
    both_fall = jnp.stack([fall_table, jnp.zeros_like(fall_table)])
    diffusion = table_lookup(level_class, kappa_table)
    falling = table_lookup(level_class, both_fall)
    global_level = my_layer * levels + jnp.arange(levels, dtype=jnp.int32)
    diffusion = jnp.where(global_level >= 1, diffusion, 0.0)
    above_class = passed_along(settle_class[:, :1], "gz", -1)
    at_top = my_layer == layers - 1
    diffusion_above = jnp.where(at_top, 0.0, table_lookup(above_class, kappa_table))
    fall_above = jnp.where(at_top, 0.0, table_lookup(above_class, both_fall))
    diffusion_up = jnp.concatenate([diffusion[..., 1:], diffusion_above], axis=-1)
    fall_up = jnp.concatenate([falling[..., 1:], fall_above], axis=-1)
    diagonal = 1.0 + diffusion + diffusion_up + falling
    lower_band = -diffusion
    upper_band = -(diffusion_up + fall_up)
    level_index = jnp.arange(levels, dtype=jnp.int32)
    block_lower = jnp.where(level_index == 0, 0.0, lower_band)
    block_upper = jnp.where(level_index == levels - 1, 0.0, upper_band)
    fields = jnp.stack([concentration, turbulence], axis=1)
    wanted = lax.all_to_all(requests, "gy", split_axis=0, concat_axis=0, tiled=True)

    def exchange(tiles):
        sent = lax.all_to_all(tiles[wanted], "gy", split_axis=0, concat_axis=0, tiled=True)
        return sent.reshape((-1,) + tiles.shape[1:])

    arrived = exchange(fields)
    inverse, wanted = block_inverse(block_lower, diagonal, block_upper, wanted)
    spike_column = jnp.where(
        my_layer == 0,
        upper_band[..., -1:] * inverse[..., :, levels - 1],
        lower_band[..., :1] * inverse[..., :, 0],
    )
    edge_spike = jnp.where(my_layer == 0, spike_column[..., -1], spike_column[..., 0])
    other_spike = from_partner(edge_spike, "gz", 0)
    low_spike = jnp.where(my_layer == 0, edge_spike, other_spike)
    high_spike = jnp.where(my_layer == 0, other_spike, edge_spike)
    ratios = []
    for step_index in range(STEPS):
        tile_pool = jnp.concatenate([fields, arrived], axis=0)
        advected = jnp.zeros(fields.shape, jnp.float32)
        for entry_k in range(sources_per):
            advected = advected + jnp.einsum(
                "tcd,tfdz->tfcz",
                interp_weights[:, entry_k],
                tile_pool[pool_index[:, entry_k]],
                preferred_element_type=jnp.float32,
            )
        last = step_index + 1 == STEPS
        totals = butterfly_sum(
            jnp.stack([jnp.sum(fields[:, 0], dtype=jnp.float32), jnp.sum(advected[:, 0])]),
            ("gz", "gy", "gx"),
        )
        solved = jnp.einsum(
            "tfzy,tfcy->tfcz",
            inverse,
            advected,
            precision=HIGHEST,
            preferred_element_type=jnp.float32,
        )
        edge_value = jnp.where(my_layer == 0, solved[..., -1], solved[..., 0])
        other_value = from_partner(edge_value, "gz", 0)
        low_value = jnp.where(my_layer == 0, edge_value, other_value)
        high_value = jnp.where(my_layer == 0, other_value, edge_value)
        lower_end, upper_end = interface_values(low_value, low_spike, high_value, high_spike)
        needed = jnp.where(my_layer == 0, upper_end, lower_end)
        unscaled = solved - spike_column[:, :, None, :] * needed[..., None]
        next_turbulence = unscaled[:, 1].astype(jnp.bfloat16)
        if not last:
            arrived_turbulence = exchange(next_turbulence)
        mass_fixer = totals[0] / totals[1]
        ratios.append(mass_fixer)
        next_concentration = (mass_fixer * unscaled[:, 0]).astype(jnp.bfloat16)
        if not last:
            arrived = jnp.stack([exchange(next_concentration), arrived_turbulence], axis=1)
        fields = jnp.stack([next_concentration, next_turbulence], axis=1)
    return (fields[:, 0], fields[:, 1], jnp.stack(ratios))


def solution(mesh):
    return jax.shard_map(
        per_device,
        mesh=mesh,
        in_specs=(
            P(("gx", "gy"), None, "gz"),
            P(("gx", "gy"), None, "gz"),
            P(("gx", "gy"), None),
            P(("gx", "gy"), None, None, None),
            P(("gx", "gy"), "gz"),
            P(),
            P(),
        ),
        out_specs=(P(("gx", "gy"), None, "gz"), P(("gx", "gy"), None, "gz"), P()),
        check_vma=False,
    )
```

```python
import jax
import jax.numpy as jnp
from jax import lax
from jax.sharding import PartitionSpec as P
from jax.experimental import pallas as pl
from jax.experimental.pallas import tpu as pltpu

STEPS = 2


HIGHEST = lax.Precision.HIGHEST


def passed_along(array, axis, by):
    devices = lax.axis_size(axis)
    pairs = [(i, i + by) for i in range(devices) if 0 <= i + by < devices]
    return lax.ppermute(array, axis, pairs)


def from_partner(array, axis, apart):
    return lax.ppermute(array, axis, [(i, i ^ 1 << apart) for i in range(lax.axis_size(axis))])


def butterfly_sum(value, axes):
    for axis in axes:
        devices = lax.axis_size(axis)
        if devices & (devices - 1):
            value = lax.psum(value, axis)
            continue
        bit = 1
        while bit < devices:
            value = value + lax.ppermute(value, axis, [(i, i ^ bit) for i in range(devices)])
            bit *= 2
    return value


def bucket_ranks(owners, wanted, buckets):
    onehot = (
        (owners[..., None] == jnp.arange(buckets, dtype=jnp.int32)) & wanted[..., None]
    ).astype(jnp.int32)
    running = jnp.cumsum(onehot, axis=-2) - 1
    return jnp.sum(onehot * running, axis=-1)


def table_lookup(level_class, lookup_table):
    classes = lookup_table.shape[-1]
    onehot = (level_class[..., None] == jnp.arange(classes, dtype=jnp.int32)).astype(jnp.float32)
    return jnp.einsum("tzq,fq->tfz", onehot, lookup_table, precision=HIGHEST)


def thomas_inverse_kernel(lower_ref, diagonal_ref, upper_ref, inverse_ref, ratio_ref):
    levels = inverse_ref.shape[0]
    lane = lax.broadcasted_iota(jnp.int32, inverse_ref.shape[1:], 1)
    pivot = 1.0 / diagonal_ref[0]
    ratio = upper_ref[0] * pivot
    row = jnp.where(lane == 0, 1.0, 0.0) * pivot
    ratio_ref[0] = ratio
    inverse_ref[0] = row

    def forward(z, carry):
        ratio, row = carry
        below = lower_ref[z]
        pivot = 1.0 / (diagonal_ref[z] - below * ratio)
        ratio = upper_ref[z] * pivot
        row = (jnp.where(lane == z, 1.0, 0.0) - below * row) * pivot
        ratio_ref[z] = ratio
        inverse_ref[z] = row
        return ratio, row

    _, row = lax.fori_loop(1, levels, forward, (ratio, row), unroll=8)

    def backward(step, row):
        z = levels - 2 - step
        row = inverse_ref[z] - ratio_ref[z] * row
        inverse_ref[z] = row
        return row

    lax.fori_loop(0, levels - 1, backward, row, unroll=8)


def block_inverse(lower, diagonal, upper, ready):
    lead = diagonal.shape[:-1]
    levels = diagonal.shape[-1]
    systems = diagonal.size // levels

    def level_major(band):
        return jnp.transpose(band.reshape(systems, levels))[:, :, None]

    bands, ready = lax.optimization_barrier(
        ((level_major(lower), level_major(diagonal), level_major(upper)), ready)
    )
    inverse = pl.pallas_call(
        thomas_inverse_kernel,
        out_shape=jax.ShapeDtypeStruct((levels, systems, levels), jnp.float32),
        scratch_shapes=[pltpu.VMEM((levels, systems, 1), jnp.float32)],
        cost_estimate=pl.CostEstimate(
            flops=16 * levels * systems * levels,
            transcendentals=levels * systems,
            bytes_accessed=64 * levels * systems * levels,
        ),
    )(*bands)
    return jnp.transpose(inverse, (1, 2, 0)).reshape(lead + (levels, levels)), ready


def interface_values(low_value, low_spike, high_value, high_spike):
    lower_end = (low_value - low_spike[..., None] * high_value) / (1.0 - low_spike * high_spike)[
        ..., None
    ]
    upper_end = high_value - high_spike[..., None] * lower_end
    return (lower_end, upper_end)


def per_device(
    concentration, turbulence, src_list, interp_weights, settle_class, kappa_table, fall_table
):
    tiles_here, columns, levels = concentration.shape
    sources_per = src_list.shape[1]
    lane_count = lax.axis_size("gy")
    my_lane = lax.axis_index("gy")
    layers = lax.axis_size("gz")
    my_layer = lax.axis_index("gz")
    remote_count = tiles_here // 2
    capacity = max(2, 3 * remote_count // (2 * (lane_count - 1)))
    entries = src_list.reshape(-1)
    owner_lane = entries // tiles_here % lane_count
    local_tile = entries % tiles_here
    remote = owner_lane != my_lane
    slot_index = bucket_ranks(owner_lane, remote, lane_count)
    match = (
        remote[None, None, :]
        & (owner_lane[None, None, :] == jnp.arange(lane_count, dtype=jnp.int32)[:, None, None])
        & (slot_index[None, None, :] == jnp.arange(capacity, dtype=jnp.int32)[None, :, None])
    )
    requests = jnp.sum(jnp.where(match, local_tile[None, None, :], 0), axis=-1, dtype=jnp.int32)
    pool_index = jnp.where(
        remote, tiles_here + owner_lane * capacity + slot_index, local_tile
    ).reshape(tiles_here, sources_per)
    level_class = jnp.repeat(settle_class, levels // settle_class.shape[1], axis=1)
    both_fall = jnp.stack([fall_table, jnp.zeros_like(fall_table)])
    diffusion = table_lookup(level_class, kappa_table)
    falling = table_lookup(level_class, both_fall)
    global_level = my_layer * levels + jnp.arange(levels, dtype=jnp.int32)
    diffusion = jnp.where(global_level >= 1, diffusion, 0.0)
    above_class = passed_along(settle_class[:, :1], "gz", -1)
    at_top = my_layer == layers - 1
    diffusion_above = jnp.where(at_top, 0.0, table_lookup(above_class, kappa_table))
    fall_above = jnp.where(at_top, 0.0, table_lookup(above_class, both_fall))
    diffusion_up = jnp.concatenate([diffusion[..., 1:], diffusion_above], axis=-1)
    fall_up = jnp.concatenate([falling[..., 1:], fall_above], axis=-1)
    diagonal = 1.0 + diffusion + diffusion_up + falling
    lower_band = -diffusion
    upper_band = -(diffusion_up + fall_up)
    level_index = jnp.arange(levels, dtype=jnp.int32)
    block_lower = jnp.where(level_index == 0, 0.0, lower_band)
    block_upper = jnp.where(level_index == levels - 1, 0.0, upper_band)
    fields = jnp.stack([concentration, turbulence], axis=1)
    wanted = lax.all_to_all(requests, "gy", split_axis=0, concat_axis=0, tiled=True)

    def exchange(tiles):
        sent = lax.all_to_all(tiles[wanted], "gy", split_axis=0, concat_axis=0, tiled=True)
        return sent.reshape((-1,) + tiles.shape[1:])

    arrived = exchange(fields)
    inverse, wanted = block_inverse(block_lower, diagonal, block_upper, wanted)
    spike_column = jnp.where(
        my_layer == 0,
        upper_band[..., -1:] * inverse[..., levels - 1, :],
        lower_band[..., :1] * inverse[..., 0, :],
    )
    edge_spike = jnp.where(my_layer == 0, spike_column[..., -1], spike_column[..., 0])
    other_spike = from_partner(edge_spike, "gz", 0)
    low_spike = jnp.where(my_layer == 0, edge_spike, other_spike)
    high_spike = jnp.where(my_layer == 0, other_spike, edge_spike)
    ratios = []
    for step_index in range(STEPS):
        tile_pool = jnp.concatenate([fields, arrived], axis=0)
        advected = jnp.zeros(fields.shape, jnp.float32)
        for entry_k in range(sources_per):
            advected = advected + jnp.einsum(
                "tcd,tfdz->tfcz",
                interp_weights[:, entry_k],
                tile_pool[pool_index[:, entry_k]],
                preferred_element_type=jnp.float32,
            )
        last = step_index + 1 == STEPS
        partial = jnp.where(
            lax.broadcasted_iota(jnp.int32, (128,), 0) == 0,
            jnp.sum(fields[:, 0], dtype=jnp.float32),
            jnp.sum(advected[:, 0]),
        )
        solved = jnp.einsum(
            "tfcy,tfyz->tfcz",
            advected,
            inverse,
            precision=HIGHEST,
            preferred_element_type=jnp.float32,
        )
        edge_value = jnp.where(my_layer == 0, solved[..., -1], solved[..., 0])
        carried = from_partner(jnp.concatenate([edge_value.reshape(-1), partial]), "gz", 0)
        other_value = carried[: edge_value.size].reshape(edge_value.shape)
        totals = butterfly_sum(partial + carried[edge_value.size :], ("gy", "gx"))
        low_value = jnp.where(my_layer == 0, edge_value, other_value)
        high_value = jnp.where(my_layer == 0, other_value, edge_value)
        lower_end, upper_end = interface_values(low_value, low_spike, high_value, high_spike)
        needed = jnp.where(my_layer == 0, upper_end, lower_end)
        unscaled = solved - spike_column[:, :, None, :] * needed[..., None]
        next_turbulence = unscaled[:, 1].astype(jnp.bfloat16)
        if not last:
            arrived_turbulence = exchange(next_turbulence)
        mass_fixer = totals[0] / totals[1]
        ratios.append(mass_fixer)
        next_concentration = (mass_fixer * unscaled[:, 0]).astype(jnp.bfloat16)
        if not last:
            arrived = jnp.stack([exchange(next_concentration), arrived_turbulence], axis=1)
        fields = jnp.stack([next_concentration, next_turbulence], axis=1)
    return (fields[:, 0], fields[:, 1], jnp.stack(ratios))


def solution(mesh):
    return jax.shard_map(
        per_device,
        mesh=mesh,
        in_specs=(
            P(("gx", "gy"), None, "gz"),
            P(("gx", "gy"), None, "gz"),
            P(("gx", "gy"), None),
            P(("gx", "gy"), None, None, None),
            P(("gx", "gy"), "gz"),
            P(),
            P(),
        ),
        out_specs=(P(("gx", "gy"), None, "gz"), P(("gx", "gy"), None, "gz"), P()),
        check_vma=False,
    )
```

```python
import jax
import jax.numpy as jnp
from jax import lax
from jax.sharding import PartitionSpec as P
from jax.experimental import pallas as pl
from jax.experimental.pallas import tpu as pltpu
from jax.experimental.layout import Layout, with_layout_constraint

STEPS = 2


HIGHEST = lax.Precision.HIGHEST


def passed_along(array, axis, by):
    devices = lax.axis_size(axis)
    pairs = [(i, i + by) for i in range(devices) if 0 <= i + by < devices]
    return lax.ppermute(array, axis, pairs)


def from_partner(array, axis, apart):
    return lax.ppermute(array, axis, [(i, i ^ 1 << apart) for i in range(lax.axis_size(axis))])


def butterfly_sum(value, axes):
    for axis in axes:
        devices = lax.axis_size(axis)
        if devices & (devices - 1):
            value = lax.psum(value, axis)
            continue
        bit = 1
        while bit < devices:
            value = value + lax.ppermute(value, axis, [(i, i ^ bit) for i in range(devices)])
            bit *= 2
    return value


def bucket_ranks(owners, wanted, buckets):
    onehot = (
        (owners[..., None] == jnp.arange(buckets, dtype=jnp.int32)) & wanted[..., None]
    ).astype(jnp.int32)
    running = jnp.cumsum(onehot, axis=-2) - 1
    return jnp.sum(onehot * running, axis=-1)


def table_lookup(level_class, lookup_table):
    classes = lookup_table.shape[-1]
    onehot = (level_class[..., None] == jnp.arange(classes, dtype=jnp.int32)).astype(jnp.float32)
    return jnp.einsum("tzq,fq->tfz", onehot, lookup_table, precision=HIGHEST)


def thomas_inverse_kernel(lower_ref, diagonal_ref, upper_ref, inverse_ref, ratio_ref):
    levels = inverse_ref.shape[0]
    lane = lax.broadcasted_iota(jnp.int32, inverse_ref.shape[1:], 1)
    pivot = 1.0 / diagonal_ref[0]
    ratio = upper_ref[0] * pivot
    row = jnp.where(lane == 0, 1.0, 0.0) * pivot
    ratio_ref[0] = ratio
    inverse_ref[0] = row

    def forward(z, carry):
        ratio, row = carry
        below = lower_ref[z]
        pivot = 1.0 / (diagonal_ref[z] - below * ratio)
        ratio = upper_ref[z] * pivot
        row = (jnp.where(lane == z, 1.0, 0.0) - below * row) * pivot
        ratio_ref[z] = ratio
        inverse_ref[z] = row
        return ratio, row

    _, row = lax.fori_loop(1, levels, forward, (ratio, row), unroll=8)

    def backward(step, row):
        z = levels - 2 - step
        row = inverse_ref[z] - ratio_ref[z] * row
        inverse_ref[z] = row
        return row

    lax.fori_loop(0, levels - 1, backward, row, unroll=8)


def block_inverse(lower, diagonal, upper, ready):
    lead = diagonal.shape[:-1]
    levels = diagonal.shape[-1]
    systems = diagonal.size // levels

    def level_major(band):
        return jnp.transpose(band.reshape(systems, levels))[:, :, None]

    bands, ready = lax.optimization_barrier(
        ((level_major(lower), level_major(diagonal), level_major(upper)), ready)
    )
    inverse = pl.pallas_call(
        thomas_inverse_kernel,
        out_shape=jax.ShapeDtypeStruct((levels, systems, levels), jnp.float32),
        scratch_shapes=[pltpu.VMEM((levels, systems, 1), jnp.float32)],
        cost_estimate=pl.CostEstimate(
            flops=16 * levels * systems * levels,
            transcendentals=levels * systems,
            bytes_accessed=64 * levels * systems * levels,
        ),
    )(*bands)
    return jnp.transpose(inverse, (1, 0, 2)).reshape(lead + (levels, levels)), ready


def interface_values(low_value, low_spike, high_value, high_spike):
    lower_end = (low_value - low_spike[..., None] * high_value) / (1.0 - low_spike * high_spike)[
        ..., None
    ]
    upper_end = high_value - high_spike[..., None] * lower_end
    return (lower_end, upper_end)


def per_device(
    concentration, turbulence, src_list, interp_weights, settle_class, kappa_table, fall_table
):
    tiles_here, columns, levels = concentration.shape
    sources_per = src_list.shape[1]
    lane_count = lax.axis_size("gy")
    my_lane = lax.axis_index("gy")
    layers = lax.axis_size("gz")
    my_layer = lax.axis_index("gz")
    remote_count = tiles_here // 2
    capacity = max(2, 3 * remote_count // (2 * (lane_count - 1)))
    entries = src_list.reshape(-1)
    owner_lane = entries // tiles_here % lane_count
    local_tile = entries % tiles_here
    remote = owner_lane != my_lane
    slot_index = bucket_ranks(owner_lane, remote, lane_count)
    match = (
        remote[None, None, :]
        & (owner_lane[None, None, :] == jnp.arange(lane_count, dtype=jnp.int32)[:, None, None])
        & (slot_index[None, None, :] == jnp.arange(capacity, dtype=jnp.int32)[None, :, None])
    )
    requests = jnp.sum(jnp.where(match, local_tile[None, None, :], 0), axis=-1, dtype=jnp.int32)
    pool_index = jnp.where(
        remote, tiles_here + owner_lane * capacity + slot_index, local_tile
    ).reshape(tiles_here, sources_per)
    level_class = jnp.repeat(settle_class, levels // settle_class.shape[1], axis=1)
    both_fall = jnp.stack([fall_table, jnp.zeros_like(fall_table)])
    diffusion = table_lookup(level_class, kappa_table)
    falling = table_lookup(level_class, both_fall)
    global_level = my_layer * levels + jnp.arange(levels, dtype=jnp.int32)
    diffusion = jnp.where(global_level >= 1, diffusion, 0.0)
    above_class = passed_along(settle_class[:, :1], "gz", -1)
    at_top = my_layer == layers - 1
    diffusion_above = jnp.where(at_top, 0.0, table_lookup(above_class, kappa_table))
    fall_above = jnp.where(at_top, 0.0, table_lookup(above_class, both_fall))
    diffusion_up = jnp.concatenate([diffusion[..., 1:], diffusion_above], axis=-1)
    fall_up = jnp.concatenate([falling[..., 1:], fall_above], axis=-1)
    diagonal = 1.0 + diffusion + diffusion_up + falling
    lower_band = -diffusion
    upper_band = -(diffusion_up + fall_up)
    level_index = jnp.arange(levels, dtype=jnp.int32)
    block_lower = jnp.where(level_index == 0, 0.0, lower_band)
    block_upper = jnp.where(level_index == levels - 1, 0.0, upper_band)
    fields = jnp.stack([concentration, turbulence], axis=1)
    wanted = lax.all_to_all(requests, "gy", split_axis=0, concat_axis=0, tiled=True)

    def exchange(tiles):
        sent = lax.all_to_all(tiles[wanted], "gy", split_axis=0, concat_axis=0, tiled=True)
        return sent.reshape((-1,) + tiles.shape[1:])

    arrived = exchange(fields)
    inverse, wanted = block_inverse(block_lower, diagonal, block_upper, wanted)
    spike_column = jnp.where(
        my_layer == 0,
        upper_band[..., -1:] * inverse[..., :, levels - 1],
        lower_band[..., :1] * inverse[..., :, 0],
    )
    edge_spike = jnp.where(my_layer == 0, spike_column[..., -1], spike_column[..., 0])
    other_spike = from_partner(edge_spike, "gz", 0)
    low_spike = jnp.where(my_layer == 0, edge_spike, other_spike)
    high_spike = jnp.where(my_layer == 0, other_spike, edge_spike)
    ratios = []
    for step_index in range(STEPS):
        tile_pool = jnp.concatenate([fields, arrived], axis=0)
        advected = jnp.zeros(fields.shape, jnp.float32)
        for entry_k in range(sources_per):
            advected = advected + jnp.einsum(
                "tcd,tfdz->tfcz",
                interp_weights[:, entry_k],
                tile_pool[pool_index[:, entry_k]],
                preferred_element_type=jnp.float32,
            )
        last = step_index + 1 == STEPS
        totals = butterfly_sum(
            jnp.stack([jnp.sum(fields[:, 0], dtype=jnp.float32), jnp.sum(advected[:, 0])]),
            ("gz", "gy", "gx"),
        )
        solved = jnp.einsum(
            "tfzy,tfcy->tfcz",
            inverse,
            advected,
            precision=HIGHEST,
            preferred_element_type=jnp.float32,
        )
        solved = with_layout_constraint(solved, Layout((0, 1, 2, 3)))
        edge_value = jnp.where(my_layer == 0, solved[..., -1], solved[..., 0])
        other_value = from_partner(edge_value, "gz", 0)
        low_value = jnp.where(my_layer == 0, edge_value, other_value)
        high_value = jnp.where(my_layer == 0, other_value, edge_value)
        lower_end, upper_end = interface_values(low_value, low_spike, high_value, high_spike)
        needed = jnp.where(my_layer == 0, upper_end, lower_end)
        unscaled = solved - spike_column[:, :, None, :] * needed[..., None]
        next_turbulence = unscaled[:, 1].astype(jnp.bfloat16)
        if not last:
            arrived_turbulence = exchange(next_turbulence)
        mass_fixer = totals[0] / totals[1]
        ratios.append(mass_fixer)
        next_concentration = (mass_fixer * unscaled[:, 0]).astype(jnp.bfloat16)
        if not last:
            arrived = jnp.stack([exchange(next_concentration), arrived_turbulence], axis=1)
        fields = jnp.stack([next_concentration, next_turbulence], axis=1)
    return (fields[:, 0], fields[:, 1], jnp.stack(ratios))


def solution(mesh):
    return jax.shard_map(
        per_device,
        mesh=mesh,
        in_specs=(
            P(("gx", "gy"), None, "gz"),
            P(("gx", "gy"), None, "gz"),
            P(("gx", "gy"), None),
            P(("gx", "gy"), None, None, None),
            P(("gx", "gy"), "gz"),
            P(),
            P(),
        ),
        out_specs=(P(("gx", "gy"), None, "gz"), P(("gx", "gy"), None, "gz"), P()),
        check_vma=False,
    )
```

```python
import jax
import jax.numpy as jnp
from jax import lax
from jax.sharding import PartitionSpec as P
from jax.experimental import pallas as pl
from jax.experimental.pallas import tpu as pltpu

STEPS = 2


HIGHEST = lax.Precision.HIGHEST


def passed_along(array, axis, by):
    devices = lax.axis_size(axis)
    pairs = [(i, i + by) for i in range(devices) if 0 <= i + by < devices]
    return lax.ppermute(array, axis, pairs)


def from_partner(array, axis, apart):
    return lax.ppermute(array, axis, [(i, i ^ 1 << apart) for i in range(lax.axis_size(axis))])


def butterfly_sum(value, axes):
    for axis in axes:
        devices = lax.axis_size(axis)
        if devices & (devices - 1):
            value = lax.psum(value, axis)
            continue
        bit = 1
        while bit < devices:
            value = value + lax.ppermute(value, axis, [(i, i ^ bit) for i in range(devices)])
            bit *= 2
    return value


def bucket_ranks(owners, wanted, buckets):
    onehot = (
        (owners[..., None] == jnp.arange(buckets, dtype=jnp.int32)) & wanted[..., None]
    ).astype(jnp.int32)
    running = jnp.cumsum(onehot, axis=-2) - 1
    return jnp.sum(onehot * running, axis=-1)


def table_lookup(level_class, lookup_table):
    classes = lookup_table.shape[-1]
    onehot = (level_class[..., None] == jnp.arange(classes, dtype=jnp.int32)).astype(jnp.float32)
    return jnp.einsum("tzq,fq->tfz", onehot, lookup_table, precision=HIGHEST)


def thomas_inverse_kernel(lower_ref, diagonal_ref, upper_ref, inverse_ref, ratio_ref):
    levels = inverse_ref.shape[0]
    lane = lax.broadcasted_iota(jnp.int32, inverse_ref.shape[1:], 1)
    pivot = 1.0 / diagonal_ref[0]
    ratio = upper_ref[0] * pivot
    row = jnp.where(lane == 0, 1.0, 0.0) * pivot
    ratio_ref[0] = ratio
    inverse_ref[0] = row

    def forward(z, carry):
        ratio, row = carry
        below = lower_ref[z]
        pivot = 1.0 / (diagonal_ref[z] - below * ratio)
        ratio = upper_ref[z] * pivot
        row = (jnp.where(lane == z, 1.0, 0.0) - below * row) * pivot
        ratio_ref[z] = ratio
        inverse_ref[z] = row
        return ratio, row

    _, row = lax.fori_loop(1, levels, forward, (ratio, row), unroll=8)

    def backward(step, row):
        z = levels - 2 - step
        row = inverse_ref[z] - ratio_ref[z] * row
        inverse_ref[z] = row
        return row

    lax.fori_loop(0, levels - 1, backward, row, unroll=8)


def block_inverse(lower, diagonal, upper, ready):
    lead = diagonal.shape[:-1]
    levels = diagonal.shape[-1]
    systems = diagonal.size // levels

    def level_major(band):
        return jnp.broadcast_to(
            jnp.transpose(band.reshape(systems, levels))[:, :, None], (levels, systems, levels)
        )

    bands, ready = lax.optimization_barrier(
        ((level_major(lower), level_major(diagonal), level_major(upper)), ready)
    )
    inverse = pl.pallas_call(
        thomas_inverse_kernel,
        out_shape=jax.ShapeDtypeStruct((levels, systems, levels), jnp.float32),
        scratch_shapes=[pltpu.VMEM((levels, systems, levels), jnp.float32)],
        cost_estimate=pl.CostEstimate(
            flops=16 * levels * systems * levels,
            transcendentals=levels * systems,
            bytes_accessed=64 * levels * systems * levels,
        ),
    )(*bands)
    return jnp.transpose(inverse, (1, 0, 2)).reshape(lead + (levels, levels)), ready


def interface_values(low_value, low_spike, high_value, high_spike):
    lower_end = (low_value - low_spike[..., None] * high_value) / (1.0 - low_spike * high_spike)[
        ..., None
    ]
    upper_end = high_value - high_spike[..., None] * lower_end
    return (lower_end, upper_end)


def per_device(
    concentration, turbulence, src_list, interp_weights, settle_class, kappa_table, fall_table
):
    tiles_here, columns, levels = concentration.shape
    sources_per = src_list.shape[1]
    lane_count = lax.axis_size("gy")
    my_lane = lax.axis_index("gy")
    layers = lax.axis_size("gz")
    my_layer = lax.axis_index("gz")
    remote_count = tiles_here // 2
    capacity = max(2, 3 * remote_count // (2 * (lane_count - 1)))
    entries = src_list.reshape(-1)
    owner_lane = entries // tiles_here % lane_count
    local_tile = entries % tiles_here
    remote = owner_lane != my_lane
    slot_index = bucket_ranks(owner_lane, remote, lane_count)
    match = (
        remote[None, None, :]
        & (owner_lane[None, None, :] == jnp.arange(lane_count, dtype=jnp.int32)[:, None, None])
        & (slot_index[None, None, :] == jnp.arange(capacity, dtype=jnp.int32)[None, :, None])
    )
    requests = jnp.sum(jnp.where(match, local_tile[None, None, :], 0), axis=-1, dtype=jnp.int32)
    pool_index = jnp.where(
        remote, tiles_here + owner_lane * capacity + slot_index, local_tile
    ).reshape(tiles_here, sources_per)
    level_class = jnp.repeat(settle_class, levels // settle_class.shape[1], axis=1)
    both_fall = jnp.stack([fall_table, jnp.zeros_like(fall_table)])
    diffusion = table_lookup(level_class, kappa_table)
    falling = table_lookup(level_class, both_fall)
    global_level = my_layer * levels + jnp.arange(levels, dtype=jnp.int32)
    diffusion = jnp.where(global_level >= 1, diffusion, 0.0)
    above_class = passed_along(settle_class[:, :1], "gz", -1)
    at_top = my_layer == layers - 1
    diffusion_above = jnp.where(at_top, 0.0, table_lookup(above_class, kappa_table))
    fall_above = jnp.where(at_top, 0.0, table_lookup(above_class, both_fall))
    diffusion_up = jnp.concatenate([diffusion[..., 1:], diffusion_above], axis=-1)
    fall_up = jnp.concatenate([falling[..., 1:], fall_above], axis=-1)
    diagonal = 1.0 + diffusion + diffusion_up + falling
    lower_band = -diffusion
    upper_band = -(diffusion_up + fall_up)
    level_index = jnp.arange(levels, dtype=jnp.int32)
    block_lower = jnp.where(level_index == 0, 0.0, lower_band)
    block_upper = jnp.where(level_index == levels - 1, 0.0, upper_band)
    fields = jnp.stack([concentration, turbulence], axis=1)
    wanted = lax.all_to_all(requests, "gy", split_axis=0, concat_axis=0, tiled=True)

    def exchange(tiles):
        sent = lax.all_to_all(tiles[wanted], "gy", split_axis=0, concat_axis=0, tiled=True)
        return sent.reshape((-1,) + tiles.shape[1:])

    arrived = exchange(fields)
    inverse, wanted = block_inverse(block_lower, diagonal, block_upper, wanted)
    coupled = lax.broadcasted_iota(jnp.int32, (levels,), 0) == jnp.where(
        my_layer == 0, levels - 1, 0
    )
    inverse_column = jnp.sum(jnp.where(coupled, inverse, 0.0), axis=-1)
    spike_column = (
        jnp.where(my_layer == 0, upper_band[..., -1:], lower_band[..., :1]) * inverse_column
    )
    edge_spike = jnp.where(my_layer == 0, spike_column[..., -1], spike_column[..., 0])
    other_spike = from_partner(edge_spike, "gz", 0)
    low_spike = jnp.where(my_layer == 0, edge_spike, other_spike)
    high_spike = jnp.where(my_layer == 0, other_spike, edge_spike)
    ratios = []
    for step_index in range(STEPS):
        tile_pool = jnp.concatenate([fields, arrived], axis=0)
        advected = jnp.zeros(fields.shape, jnp.float32)
        for entry_k in range(sources_per):
            advected = advected + jnp.einsum(
                "tcd,tfdz->tfcz",
                interp_weights[:, entry_k],
                tile_pool[pool_index[:, entry_k]],
                preferred_element_type=jnp.float32,
            )
        last = step_index + 1 == STEPS
        totals = butterfly_sum(
            jnp.stack([jnp.sum(fields[:, 0], dtype=jnp.float32), jnp.sum(advected[:, 0])]),
            ("gz", "gy", "gx"),
        )
        solved = jnp.einsum(
            "tfzy,tfcy->tfcz",
            inverse,
            advected,
            precision=HIGHEST,
            preferred_element_type=jnp.float32,
        )
        edge_value = jnp.where(my_layer == 0, solved[..., -1], solved[..., 0])
        other_value = from_partner(edge_value, "gz", 0)
        low_value = jnp.where(my_layer == 0, edge_value, other_value)
        high_value = jnp.where(my_layer == 0, other_value, edge_value)
        lower_end, upper_end = interface_values(low_value, low_spike, high_value, high_spike)
        needed = jnp.where(my_layer == 0, upper_end, lower_end)
        unscaled = solved - spike_column[:, :, None, :] * needed[..., None]
        next_turbulence = unscaled[:, 1].astype(jnp.bfloat16)
        if not last:
            arrived_turbulence = exchange(next_turbulence)
        mass_fixer = totals[0] / totals[1]
        ratios.append(mass_fixer)
        next_concentration = (mass_fixer * unscaled[:, 0]).astype(jnp.bfloat16)
        if not last:
            arrived = jnp.stack([exchange(next_concentration), arrived_turbulence], axis=1)
        fields = jnp.stack([next_concentration, next_turbulence], axis=1)
    return (fields[:, 0], fields[:, 1], jnp.stack(ratios))


def solution(mesh):
    return jax.shard_map(
        per_device,
        mesh=mesh,
        in_specs=(
            P(("gx", "gy"), None, "gz"),
            P(("gx", "gy"), None, "gz"),
            P(("gx", "gy"), None),
            P(("gx", "gy"), None, None, None),
            P(("gx", "gy"), "gz"),
            P(),
            P(),
        ),
        out_specs=(P(("gx", "gy"), None, "gz"), P(("gx", "gy"), None, "gz"), P()),
        check_vma=False,
    )
```

```python
import jax
import jax.numpy as jnp
from jax import lax
from jax.sharding import PartitionSpec as P
from jax.experimental import pallas as pl
from jax.experimental.pallas import tpu as pltpu

STEPS = 2


HIGHEST = lax.Precision.HIGHEST


def passed_along(array, axis, by):
    devices = lax.axis_size(axis)
    pairs = [(i, i + by) for i in range(devices) if 0 <= i + by < devices]
    return lax.ppermute(array, axis, pairs)


def from_partner(array, axis, apart):
    return lax.ppermute(array, axis, [(i, i ^ 1 << apart) for i in range(lax.axis_size(axis))])


def butterfly_sum(value, axes):
    for axis in axes:
        devices = lax.axis_size(axis)
        if devices & (devices - 1):
            value = lax.psum(value, axis)
            continue
        bit = 1
        while bit < devices:
            value = value + lax.ppermute(value, axis, [(i, i ^ bit) for i in range(devices)])
            bit *= 2
    return value


def bucket_ranks(owners, wanted, buckets):
    onehot = (
        (owners[..., None] == jnp.arange(buckets, dtype=jnp.int32)) & wanted[..., None]
    ).astype(jnp.int32)
    running = jnp.cumsum(onehot, axis=-2) - 1
    return jnp.sum(onehot * running, axis=-1)


def table_lookup(level_class, lookup_table):
    classes = lookup_table.shape[-1]
    onehot = (level_class[..., None] == jnp.arange(classes, dtype=jnp.int32)).astype(jnp.float32)
    return jnp.einsum("tzq,fq->tfz", onehot, lookup_table, precision=HIGHEST)


def thomas_inverse_kernel(lower_ref, diagonal_ref, upper_ref, inverse_ref, ratio_ref):
    levels = inverse_ref.shape[0]
    lane = lax.broadcasted_iota(jnp.int32, inverse_ref.shape[1:], 1)
    pivot = 1.0 / diagonal_ref[0]
    ratio = upper_ref[0] * pivot
    row = jnp.where(lane == 0, 1.0, 0.0) * pivot
    ratio_ref[0] = ratio
    inverse_ref[0] = row

    def forward(z, carry):
        ratio, row = carry
        below = lower_ref[z]
        pivot = 1.0 / (diagonal_ref[z] - below * ratio)
        ratio = upper_ref[z] * pivot
        row = (jnp.where(lane == z, 1.0, 0.0) - below * row) * pivot
        ratio_ref[z] = ratio
        inverse_ref[z] = row
        return ratio, row

    _, row = lax.fori_loop(1, levels, forward, (ratio, row), unroll=8)

    def backward(step, row):
        z = levels - 2 - step
        row = inverse_ref[z] - ratio_ref[z] * row
        inverse_ref[z] = row
        return row

    lax.fori_loop(0, levels - 1, backward, row, unroll=8)


def block_inverse(lower, diagonal, upper, ready):
    lead = diagonal.shape[:-1]
    levels = diagonal.shape[-1]
    systems = diagonal.size // levels

    def level_major(band):
        return jnp.broadcast_to(
            jnp.transpose(band.reshape(systems, levels))[:, :, None], (levels, systems, levels)
        )

    bands, ready = lax.optimization_barrier(
        ((level_major(lower), level_major(diagonal), level_major(upper)), ready)
    )
    inverse = pl.pallas_call(
        thomas_inverse_kernel,
        out_shape=jax.ShapeDtypeStruct((levels, systems, levels), jnp.float32),
        scratch_shapes=[pltpu.VMEM((levels, systems, levels), jnp.float32)],
        cost_estimate=pl.CostEstimate(
            flops=16 * levels * systems * levels,
            transcendentals=levels * systems,
            bytes_accessed=64 * levels * systems * levels,
        ),
    )(*bands)
    return jnp.transpose(inverse, (1, 0, 2)).reshape(lead + (levels, levels)), ready


def interface_values(low_value, low_spike, high_value, high_spike):
    lower_end = (low_value - low_spike[..., None] * high_value) / (1.0 - low_spike * high_spike)[
        ..., None
    ]
    upper_end = high_value - high_spike[..., None] * lower_end
    return (lower_end, upper_end)


def per_device(
    concentration, turbulence, src_list, interp_weights, settle_class, kappa_table, fall_table
):
    tiles_here, columns, levels = concentration.shape
    sources_per = src_list.shape[1]
    lane_count = lax.axis_size("gy")
    my_lane = lax.axis_index("gy")
    layers = lax.axis_size("gz")
    my_layer = lax.axis_index("gz")
    remote_count = tiles_here // 2
    capacity = max(2, 3 * remote_count // (2 * (lane_count - 1)))
    entries = src_list.reshape(-1)
    owner_lane = entries // tiles_here % lane_count
    local_tile = entries % tiles_here
    remote = owner_lane != my_lane
    slot_index = bucket_ranks(owner_lane, remote, lane_count)
    match = (
        remote[None, None, :]
        & (owner_lane[None, None, :] == jnp.arange(lane_count, dtype=jnp.int32)[:, None, None])
        & (slot_index[None, None, :] == jnp.arange(capacity, dtype=jnp.int32)[None, :, None])
    )
    requests = jnp.sum(jnp.where(match, local_tile[None, None, :], 0), axis=-1, dtype=jnp.int32)
    entry_count = entries.shape[0]
    remote_rank = jnp.cumsum(remote.astype(jnp.int32)) - 1
    picks = remote[None, :] & (
        remote_rank[None, :] == jnp.arange(remote_count, dtype=jnp.int32)[:, None]
    )
    remote_entry = jnp.sum(
        jnp.where(picks, jnp.arange(entry_count, dtype=jnp.int32)[None, :], 0), axis=1
    )
    remote_slot = (owner_lane * capacity + slot_index)[remote_entry]
    remote_tile = remote_entry // sources_per
    remote_weights = interp_weights.reshape((entry_count,) + interp_weights.shape[2:])[
        remote_entry
    ]
    remote_owner = (
        remote_tile[None, :] == jnp.arange(tiles_here, dtype=jnp.int32)[:, None]
    ).astype(jnp.float32)
    local_index = jnp.where(remote, 0, local_tile).reshape(tiles_here, sources_per)
    local_weights = jnp.where(
        remote.reshape(tiles_here, sources_per)[:, :, None, None],
        jnp.zeros_like(interp_weights),
        interp_weights,
    )
    level_class = jnp.repeat(settle_class, levels // settle_class.shape[1], axis=1)
    both_fall = jnp.stack([fall_table, jnp.zeros_like(fall_table)])
    diffusion = table_lookup(level_class, kappa_table)
    falling = table_lookup(level_class, both_fall)
    global_level = my_layer * levels + jnp.arange(levels, dtype=jnp.int32)
    diffusion = jnp.where(global_level >= 1, diffusion, 0.0)
    above_class = passed_along(settle_class[:, :1], "gz", -1)
    at_top = my_layer == layers - 1
    diffusion_above = jnp.where(at_top, 0.0, table_lookup(above_class, kappa_table))
    fall_above = jnp.where(at_top, 0.0, table_lookup(above_class, both_fall))
    diffusion_up = jnp.concatenate([diffusion[..., 1:], diffusion_above], axis=-1)
    fall_up = jnp.concatenate([falling[..., 1:], fall_above], axis=-1)
    diagonal = 1.0 + diffusion + diffusion_up + falling
    lower_band = -diffusion
    upper_band = -(diffusion_up + fall_up)
    level_index = jnp.arange(levels, dtype=jnp.int32)
    block_lower = jnp.where(level_index == 0, 0.0, lower_band)
    block_upper = jnp.where(level_index == levels - 1, 0.0, upper_band)
    fields = jnp.stack([concentration, turbulence], axis=1)
    wanted = lax.all_to_all(requests, "gy", split_axis=0, concat_axis=0, tiled=True)

    def exchange(tiles):
        sent = lax.all_to_all(tiles[wanted], "gy", split_axis=0, concat_axis=0, tiled=True)
        return sent.reshape((-1,) + tiles.shape[1:])

    arrived = exchange(fields)
    inverse, wanted = block_inverse(block_lower, diagonal, block_upper, wanted)
    coupled = lax.broadcasted_iota(jnp.int32, (levels,), 0) == jnp.where(
        my_layer == 0, levels - 1, 0
    )
    inverse_column = jnp.sum(jnp.where(coupled, inverse, 0.0), axis=-1)
    spike_column = (
        jnp.where(my_layer == 0, upper_band[..., -1:], lower_band[..., :1]) * inverse_column
    )
    edge_spike = jnp.where(my_layer == 0, spike_column[..., -1], spike_column[..., 0])
    other_spike = from_partner(edge_spike, "gz", 0)
    low_spike = jnp.where(my_layer == 0, edge_spike, other_spike)
    high_spike = jnp.where(my_layer == 0, other_spike, edge_spike)
    ratios = []
    for step_index in range(STEPS):
        advected = jnp.zeros(fields.shape, jnp.float32)
        for entry_k in range(sources_per):
            advected = advected + jnp.einsum(
                "tcd,tfdz->tfcz",
                local_weights[:, entry_k],
                fields[local_index[:, entry_k]],
                preferred_element_type=jnp.float32,
            )
        remote_terms = jnp.einsum(
            "rcd,rfdz->rfcz",
            remote_weights,
            arrived[remote_slot],
            preferred_element_type=jnp.float32,
        )
        advected = advected + jnp.einsum(
            "tr,rfcz->tfcz",
            remote_owner,
            remote_terms,
            precision=HIGHEST,
            preferred_element_type=jnp.float32,
        )
        last = step_index + 1 == STEPS
        totals = butterfly_sum(
            jnp.stack([jnp.sum(fields[:, 0], dtype=jnp.float32), jnp.sum(advected[:, 0])]),
            ("gz", "gy", "gx"),
        )
        solved = jnp.einsum(
            "tfzy,tfcy->tfcz",
            inverse,
            advected,
            precision=HIGHEST,
            preferred_element_type=jnp.float32,
        )
        edge_value = jnp.where(my_layer == 0, solved[..., -1], solved[..., 0])
        other_value = from_partner(edge_value, "gz", 0)
        low_value = jnp.where(my_layer == 0, edge_value, other_value)
        high_value = jnp.where(my_layer == 0, other_value, edge_value)
        lower_end, upper_end = interface_values(low_value, low_spike, high_value, high_spike)
        needed = jnp.where(my_layer == 0, upper_end, lower_end)
        unscaled = solved - spike_column[:, :, None, :] * needed[..., None]
        next_turbulence = unscaled[:, 1].astype(jnp.bfloat16)
        if not last:
            arrived_turbulence = exchange(next_turbulence)
        mass_fixer = totals[0] / totals[1]
        ratios.append(mass_fixer)
        next_concentration = (mass_fixer * unscaled[:, 0]).astype(jnp.bfloat16)
        if not last:
            arrived = jnp.stack([exchange(next_concentration), arrived_turbulence], axis=1)
        fields = jnp.stack([next_concentration, next_turbulence], axis=1)
    return (fields[:, 0], fields[:, 1], jnp.stack(ratios))


def solution(mesh):
    return jax.shard_map(
        per_device,
        mesh=mesh,
        in_specs=(
            P(("gx", "gy"), None, "gz"),
            P(("gx", "gy"), None, "gz"),
            P(("gx", "gy"), None),
            P(("gx", "gy"), None, None, None),
            P(("gx", "gy"), "gz"),
            P(),
            P(),
        ),
        out_specs=(P(("gx", "gy"), None, "gz"), P(("gx", "gy"), None, "gz"), P()),
        check_vma=False,
    )
```

```python
import jax
import jax.numpy as jnp
from jax import lax
from jax.sharding import PartitionSpec as P
from jax.experimental import pallas as pl
from jax.experimental.pallas import tpu as pltpu

STEPS = 2


HIGHEST = lax.Precision.HIGHEST


def passed_along(array, axis, by):
    devices = lax.axis_size(axis)
    pairs = [(i, i + by) for i in range(devices) if 0 <= i + by < devices]
    return lax.ppermute(array, axis, pairs)


def from_partner(array, axis, apart):
    return lax.ppermute(array, axis, [(i, i ^ 1 << apart) for i in range(lax.axis_size(axis))])


def butterfly_sum(value, axes):
    for axis in axes:
        devices = lax.axis_size(axis)
        if devices & (devices - 1):
            value = lax.psum(value, axis)
            continue
        bit = 1
        while bit < devices:
            value = value + lax.ppermute(value, axis, [(i, i ^ bit) for i in range(devices)])
            bit *= 2
    return value


def bucket_ranks(owners, wanted, buckets):
    onehot = (
        (owners[..., None] == jnp.arange(buckets, dtype=jnp.int32)) & wanted[..., None]
    ).astype(jnp.int32)
    running = jnp.cumsum(onehot, axis=-2) - 1
    return jnp.sum(onehot * running, axis=-1)


def table_lookup(level_class, lookup_table):
    classes = lookup_table.shape[-1]
    onehot = (level_class[..., None] == jnp.arange(classes, dtype=jnp.int32)).astype(jnp.float32)
    return jnp.einsum("tzq,fq->tfz", onehot, lookup_table, precision=HIGHEST)


def thomas_inverse_kernel(lower_ref, diagonal_ref, upper_ref, inverse_ref, ratio_ref):
    levels = inverse_ref.shape[0]
    lane = lax.broadcasted_iota(jnp.int32, inverse_ref.shape[1:], 1)
    pivot = 1.0 / diagonal_ref[0]
    ratio = upper_ref[0] * pivot
    row = jnp.where(lane == 0, 1.0, 0.0) * pivot
    ratio_ref[0] = ratio
    inverse_ref[0] = row

    def forward(z, carry):
        ratio, row = carry
        below = lower_ref[z]
        pivot = 1.0 / (diagonal_ref[z] - below * ratio)
        ratio = upper_ref[z] * pivot
        row = (jnp.where(lane == z, 1.0, 0.0) - below * row) * pivot
        ratio_ref[z] = ratio
        inverse_ref[z] = row
        return ratio, row

    _, row = lax.fori_loop(1, levels, forward, (ratio, row), unroll=8)

    def backward(step, row):
        z = levels - 2 - step
        row = inverse_ref[z] - ratio_ref[z] * row
        inverse_ref[z] = row
        return row

    lax.fori_loop(0, levels - 1, backward, row, unroll=8)


def block_inverse(lower, diagonal, upper, ready):
    lead = diagonal.shape[:-1]
    levels = diagonal.shape[-1]
    systems = diagonal.size // levels

    def level_major(band):
        return jnp.broadcast_to(
            jnp.transpose(band.reshape(systems, levels))[:, :, None], (levels, systems, levels)
        )

    bands, ready = lax.optimization_barrier(
        ((level_major(lower), level_major(diagonal), level_major(upper)), ready)
    )
    inverse = pl.pallas_call(
        thomas_inverse_kernel,
        out_shape=jax.ShapeDtypeStruct((levels, systems, levels), jnp.float32),
        scratch_shapes=[pltpu.VMEM((levels, systems, levels), jnp.float32)],
        cost_estimate=pl.CostEstimate(
            flops=16 * levels * systems * levels,
            transcendentals=levels * systems,
            bytes_accessed=64 * levels * systems * levels,
        ),
    )(*bands)
    return jnp.transpose(inverse, (1, 0, 2)).reshape(lead + (levels, levels)), ready


def advect_kernel(index_ref, weight_ref, pool_ref, out_ref):
    tiles, sources = weight_ref.shape[:2]
    fields = out_ref.shape[1]

    def one_tile(t, carry):
        picked = [index_ref[t * sources + k] for k in range(sources)]
        for field in range(fields):
            total = jnp.dot(
                weight_ref[t, 0], pool_ref[picked[0], field], preferred_element_type=jnp.float32
            )
            for k in range(1, sources):
                total = total + jnp.dot(
                    weight_ref[t, k], pool_ref[picked[k], field], preferred_element_type=jnp.float32
                )
            out_ref[t, field] = total
        return carry

    lax.fori_loop(0, tiles, one_tile, 0)


def advect(weights, tile_pool, pool_index):
    tiles, sources = pool_index.shape
    _, fields, columns, levels = tile_pool.shape
    return pl.pallas_call(
        advect_kernel,
        out_shape=jax.ShapeDtypeStruct((tiles, fields, columns, levels), jnp.float32),
        in_specs=[
            pl.BlockSpec(memory_space=pltpu.SMEM),
            pl.BlockSpec(memory_space=pltpu.VMEM),
            pl.BlockSpec(memory_space=pltpu.VMEM),
        ],
        out_specs=pl.BlockSpec(memory_space=pltpu.VMEM),
        cost_estimate=pl.CostEstimate(
            flops=2 * tiles * sources * fields * columns * columns * levels,
            transcendentals=0,
            bytes_accessed=weights.size * 2 + tile_pool.size * 2 + tiles * fields * columns * levels * 4,
        ),
    )(pool_index.reshape(-1), weights, tile_pool)


def interface_values(low_value, low_spike, high_value, high_spike):
    lower_end = (low_value - low_spike[..., None] * high_value) / (1.0 - low_spike * high_spike)[
        ..., None
    ]
    upper_end = high_value - high_spike[..., None] * lower_end
    return (lower_end, upper_end)


def per_device(
    concentration, turbulence, src_list, interp_weights, settle_class, kappa_table, fall_table
):
    tiles_here, columns, levels = concentration.shape
    sources_per = src_list.shape[1]
    lane_count = lax.axis_size("gy")
    my_lane = lax.axis_index("gy")
    layers = lax.axis_size("gz")
    my_layer = lax.axis_index("gz")
    remote_count = tiles_here // 2
    capacity = max(2, 3 * remote_count // (2 * (lane_count - 1)))
    entries = src_list.reshape(-1)
    owner_lane = entries // tiles_here % lane_count
    local_tile = entries % tiles_here
    remote = owner_lane != my_lane
    slot_index = bucket_ranks(owner_lane, remote, lane_count)
    match = (
        remote[None, None, :]
        & (owner_lane[None, None, :] == jnp.arange(lane_count, dtype=jnp.int32)[:, None, None])
        & (slot_index[None, None, :] == jnp.arange(capacity, dtype=jnp.int32)[None, :, None])
    )
    requests = jnp.sum(jnp.where(match, local_tile[None, None, :], 0), axis=-1, dtype=jnp.int32)
    pool_index = jnp.where(
        remote, tiles_here + owner_lane * capacity + slot_index, local_tile
    ).reshape(tiles_here, sources_per)
    level_class = jnp.repeat(settle_class, levels // settle_class.shape[1], axis=1)
    both_fall = jnp.stack([fall_table, jnp.zeros_like(fall_table)])
    diffusion = table_lookup(level_class, kappa_table)
    falling = table_lookup(level_class, both_fall)
    global_level = my_layer * levels + jnp.arange(levels, dtype=jnp.int32)
    diffusion = jnp.where(global_level >= 1, diffusion, 0.0)
    above_class = passed_along(settle_class[:, :1], "gz", -1)
    at_top = my_layer == layers - 1
    diffusion_above = jnp.where(at_top, 0.0, table_lookup(above_class, kappa_table))
    fall_above = jnp.where(at_top, 0.0, table_lookup(above_class, both_fall))
    diffusion_up = jnp.concatenate([diffusion[..., 1:], diffusion_above], axis=-1)
    fall_up = jnp.concatenate([falling[..., 1:], fall_above], axis=-1)
    diagonal = 1.0 + diffusion + diffusion_up + falling
    lower_band = -diffusion
    upper_band = -(diffusion_up + fall_up)
    level_index = jnp.arange(levels, dtype=jnp.int32)
    block_lower = jnp.where(level_index == 0, 0.0, lower_band)
    block_upper = jnp.where(level_index == levels - 1, 0.0, upper_band)
    fields = jnp.stack([concentration, turbulence], axis=1)
    wanted = lax.all_to_all(requests, "gy", split_axis=0, concat_axis=0, tiled=True)

    def exchange(tiles):
        sent = lax.all_to_all(tiles[wanted], "gy", split_axis=0, concat_axis=0, tiled=True)
        return sent.reshape((-1,) + tiles.shape[1:])

    arrived = exchange(fields)
    inverse, wanted = block_inverse(block_lower, diagonal, block_upper, wanted)
    coupled = lax.broadcasted_iota(jnp.int32, (levels,), 0) == jnp.where(
        my_layer == 0, levels - 1, 0
    )
    inverse_column = jnp.sum(jnp.where(coupled, inverse, 0.0), axis=-1)
    spike_column = (
        jnp.where(my_layer == 0, upper_band[..., -1:], lower_band[..., :1]) * inverse_column
    )
    edge_spike = jnp.where(my_layer == 0, spike_column[..., -1], spike_column[..., 0])
    other_spike = from_partner(edge_spike, "gz", 0)
    low_spike = jnp.where(my_layer == 0, edge_spike, other_spike)
    high_spike = jnp.where(my_layer == 0, other_spike, edge_spike)
    ratios = []
    for step_index in range(STEPS):
        tile_pool = jnp.concatenate([fields, arrived], axis=0)
        advected = advect(interp_weights, tile_pool, pool_index)
        last = step_index + 1 == STEPS
        totals = butterfly_sum(
            jnp.stack([jnp.sum(fields[:, 0], dtype=jnp.float32), jnp.sum(advected[:, 0])]),
            ("gz", "gy", "gx"),
        )
        solved = jnp.einsum(
            "tfzy,tfcy->tfcz",
            inverse,
            advected,
            precision=HIGHEST,
            preferred_element_type=jnp.float32,
        )
        edge_value = jnp.where(my_layer == 0, solved[..., -1], solved[..., 0])
        other_value = from_partner(edge_value, "gz", 0)
        low_value = jnp.where(my_layer == 0, edge_value, other_value)
        high_value = jnp.where(my_layer == 0, other_value, edge_value)
        lower_end, upper_end = interface_values(low_value, low_spike, high_value, high_spike)
        needed = jnp.where(my_layer == 0, upper_end, lower_end)
        unscaled = solved - spike_column[:, :, None, :] * needed[..., None]
        next_turbulence = unscaled[:, 1].astype(jnp.bfloat16)
        if not last:
            arrived_turbulence = exchange(next_turbulence)
        mass_fixer = totals[0] / totals[1]
        ratios.append(mass_fixer)
        next_concentration = (mass_fixer * unscaled[:, 0]).astype(jnp.bfloat16)
        if not last:
            arrived = jnp.stack([exchange(next_concentration), arrived_turbulence], axis=1)
        fields = jnp.stack([next_concentration, next_turbulence], axis=1)
    return (fields[:, 0], fields[:, 1], jnp.stack(ratios))


def solution(mesh):
    return jax.shard_map(
        per_device,
        mesh=mesh,
        in_specs=(
            P(("gx", "gy"), None, "gz"),
            P(("gx", "gy"), None, "gz"),
            P(("gx", "gy"), None),
            P(("gx", "gy"), None, None, None),
            P(("gx", "gy"), "gz"),
            P(),
            P(),
        ),
        out_specs=(P(("gx", "gy"), None, "gz"), P(("gx", "gy"), None, "gz"), P()),
        check_vma=False,
    )
```

```python
import jax
import jax.numpy as jnp
from jax import lax
from jax.sharding import PartitionSpec as P
from jax.experimental import pallas as pl
from jax.experimental.pallas import tpu as pltpu

STEPS = 2


HIGHEST = lax.Precision.HIGHEST


def passed_along(array, axis, by):
    devices = lax.axis_size(axis)
    pairs = [(i, i + by) for i in range(devices) if 0 <= i + by < devices]
    return lax.ppermute(array, axis, pairs)


def from_partner(array, axis, apart):
    return lax.ppermute(array, axis, [(i, i ^ 1 << apart) for i in range(lax.axis_size(axis))])


def butterfly_sum(value, axes):
    for axis in axes:
        devices = lax.axis_size(axis)
        if devices & (devices - 1):
            value = lax.psum(value, axis)
            continue
        bit = 1
        while bit < devices:
            value = value + lax.ppermute(value, axis, [(i, i ^ bit) for i in range(devices)])
            bit *= 2
    return value


def bucket_ranks(owners, wanted, buckets):
    onehot = (
        (owners[..., None] == jnp.arange(buckets, dtype=jnp.int32)) & wanted[..., None]
    ).astype(jnp.int32)
    running = jnp.cumsum(onehot, axis=-2) - 1
    return jnp.sum(onehot * running, axis=-1)


def table_lookup(level_class, lookup_table):
    classes = lookup_table.shape[-1]
    onehot = (level_class[..., None] == jnp.arange(classes, dtype=jnp.int32)).astype(jnp.float32)
    return jnp.einsum("tzq,fq->tfz", onehot, lookup_table, precision=HIGHEST)


def thomas_inverse_kernel(lower_ref, diagonal_ref, upper_ref, inverse_ref, ratio_ref):
    levels = inverse_ref.shape[0]
    lane = lax.broadcasted_iota(jnp.int32, inverse_ref.shape[1:], 1)
    pivot = 1.0 / diagonal_ref[0]
    ratio = upper_ref[0] * pivot
    row = jnp.where(lane == 0, 1.0, 0.0) * pivot
    ratio_ref[0] = ratio
    inverse_ref[0] = row

    def forward(z, carry):
        ratio, row = carry
        below = lower_ref[z]
        pivot = 1.0 / (diagonal_ref[z] - below * ratio)
        ratio = upper_ref[z] * pivot
        row = (jnp.where(lane == z, 1.0, 0.0) - below * row) * pivot
        ratio_ref[z] = ratio
        inverse_ref[z] = row
        return ratio, row

    _, row = lax.fori_loop(1, levels, forward, (ratio, row), unroll=8)

    def backward(step, row):
        z = levels - 2 - step
        row = inverse_ref[z] - ratio_ref[z] * row
        inverse_ref[z] = row
        return row

    lax.fori_loop(0, levels - 1, backward, row, unroll=8)


def block_inverse(lower, diagonal, upper, ready):
    lead = diagonal.shape[:-1]
    levels = diagonal.shape[-1]
    systems = diagonal.size // levels

    def level_major(band):
        return jnp.broadcast_to(
            jnp.transpose(band.reshape(systems, levels))[:, :, None], (levels, systems, levels)
        )

    bands, ready = lax.optimization_barrier(
        ((level_major(lower), level_major(diagonal), level_major(upper)), ready)
    )
    inverse = pl.pallas_call(
        thomas_inverse_kernel,
        out_shape=jax.ShapeDtypeStruct((levels, systems, levels), jnp.float32),
        scratch_shapes=[pltpu.VMEM((levels, systems, levels), jnp.float32)],
        cost_estimate=pl.CostEstimate(
            flops=16 * levels * systems * levels,
            transcendentals=levels * systems,
            bytes_accessed=64 * levels * systems * levels,
        ),
    )(*bands)
    return jnp.transpose(inverse, (1, 0, 2)).reshape(lead + (levels, levels)), ready


def advect_solve_kernel(index_ref, weight_ref, pool_ref, inverse_ref, solved_ref, sums_ref):
    tiles, sources = weight_ref.shape[:2]
    fields = solved_ref.shape[1]

    def one_tile(t, carry):
        picked = [index_ref[t * sources + k] for k in range(sources)]
        for field in range(fields):
            total = jnp.dot(
                weight_ref[t, 0], pool_ref[picked[0], field], preferred_element_type=jnp.float32
            )
            for k in range(1, sources):
                total = total + jnp.dot(
                    weight_ref[t, k], pool_ref[picked[k], field], preferred_element_type=jnp.float32
                )
            if field == 0:
                sums_ref[t] = jnp.sum(total, axis=0, keepdims=True)
            solved_ref[t, field] = lax.dot_general(
                total,
                inverse_ref[t, field],
                (((1,), (1,)), ((), ())),
                precision=HIGHEST,
                preferred_element_type=jnp.float32,
            )
        return carry

    lax.fori_loop(0, tiles, one_tile, 0)


def advect_solve(weights, tile_pool, pool_index, inverse):
    tiles, sources = pool_index.shape
    _, fields, columns, levels = tile_pool.shape
    return pl.pallas_call(
        advect_solve_kernel,
        out_shape=(
            jax.ShapeDtypeStruct((tiles, fields, columns, levels), jnp.float32),
            jax.ShapeDtypeStruct((tiles, 1, levels), jnp.float32),
        ),
        in_specs=[
            pl.BlockSpec(memory_space=pltpu.SMEM),
            pl.BlockSpec(memory_space=pltpu.VMEM),
            pl.BlockSpec(memory_space=pltpu.VMEM),
            pl.BlockSpec(memory_space=pltpu.VMEM),
        ],
        out_specs=(pl.BlockSpec(memory_space=pltpu.VMEM), pl.BlockSpec(memory_space=pltpu.VMEM)),
        cost_estimate=pl.CostEstimate(
            flops=2 * tiles * (sources + 6) * fields * columns * columns * levels,
            transcendentals=0,
            bytes_accessed=weights.size * 2 + tile_pool.size * 2 + inverse.size * 4
            + tiles * fields * columns * levels * 4,
        ),
    )(pool_index.reshape(-1), weights, tile_pool, inverse)


def interface_values(low_value, low_spike, high_value, high_spike):
    lower_end = (low_value - low_spike[..., None] * high_value) / (1.0 - low_spike * high_spike)[
        ..., None
    ]
    upper_end = high_value - high_spike[..., None] * lower_end
    return (lower_end, upper_end)


def per_device(
    concentration, turbulence, src_list, interp_weights, settle_class, kappa_table, fall_table
):
    tiles_here, columns, levels = concentration.shape
    sources_per = src_list.shape[1]
    lane_count = lax.axis_size("gy")
    my_lane = lax.axis_index("gy")
    layers = lax.axis_size("gz")
    my_layer = lax.axis_index("gz")
    remote_count = tiles_here // 2
    capacity = max(2, 3 * remote_count // (2 * (lane_count - 1)))
    entries = src_list.reshape(-1)
    owner_lane = entries // tiles_here % lane_count
    local_tile = entries % tiles_here
    remote = owner_lane != my_lane
    slot_index = bucket_ranks(owner_lane, remote, lane_count)
    match = (
        remote[None, None, :]
        & (owner_lane[None, None, :] == jnp.arange(lane_count, dtype=jnp.int32)[:, None, None])
        & (slot_index[None, None, :] == jnp.arange(capacity, dtype=jnp.int32)[None, :, None])
    )
    requests = jnp.sum(jnp.where(match, local_tile[None, None, :], 0), axis=-1, dtype=jnp.int32)
    pool_index = jnp.where(
        remote, tiles_here + owner_lane * capacity + slot_index, local_tile
    ).reshape(tiles_here, sources_per)
    level_class = jnp.repeat(settle_class, levels // settle_class.shape[1], axis=1)
    both_fall = jnp.stack([fall_table, jnp.zeros_like(fall_table)])
    diffusion = table_lookup(level_class, kappa_table)
    falling = table_lookup(level_class, both_fall)
    global_level = my_layer * levels + jnp.arange(levels, dtype=jnp.int32)
    diffusion = jnp.where(global_level >= 1, diffusion, 0.0)
    above_class = passed_along(settle_class[:, :1], "gz", -1)
    at_top = my_layer == layers - 1
    diffusion_above = jnp.where(at_top, 0.0, table_lookup(above_class, kappa_table))
    fall_above = jnp.where(at_top, 0.0, table_lookup(above_class, both_fall))
    diffusion_up = jnp.concatenate([diffusion[..., 1:], diffusion_above], axis=-1)
    fall_up = jnp.concatenate([falling[..., 1:], fall_above], axis=-1)
    diagonal = 1.0 + diffusion + diffusion_up + falling
    lower_band = -diffusion
    upper_band = -(diffusion_up + fall_up)
    level_index = jnp.arange(levels, dtype=jnp.int32)
    block_lower = jnp.where(level_index == 0, 0.0, lower_band)
    block_upper = jnp.where(level_index == levels - 1, 0.0, upper_band)
    fields = jnp.stack([concentration, turbulence], axis=1)
    wanted = lax.all_to_all(requests, "gy", split_axis=0, concat_axis=0, tiled=True)

    def exchange(tiles):
        sent = lax.all_to_all(tiles[wanted], "gy", split_axis=0, concat_axis=0, tiled=True)
        return sent.reshape((-1,) + tiles.shape[1:])

    arrived = exchange(fields)
    inverse, wanted = block_inverse(block_lower, diagonal, block_upper, wanted)
    coupled = lax.broadcasted_iota(jnp.int32, (levels,), 0) == jnp.where(
        my_layer == 0, levels - 1, 0
    )
    inverse_column = jnp.sum(jnp.where(coupled, inverse, 0.0), axis=-1)
    spike_column = (
        jnp.where(my_layer == 0, upper_band[..., -1:], lower_band[..., :1]) * inverse_column
    )
    edge_spike = jnp.where(my_layer == 0, spike_column[..., -1], spike_column[..., 0])
    other_spike = from_partner(edge_spike, "gz", 0)
    low_spike = jnp.where(my_layer == 0, edge_spike, other_spike)
    high_spike = jnp.where(my_layer == 0, other_spike, edge_spike)
    ratios = []
    for step_index in range(STEPS):
        tile_pool = jnp.concatenate([fields, arrived], axis=0)
        solved, advected_sums = advect_solve(interp_weights, tile_pool, pool_index, inverse)
        last = step_index + 1 == STEPS
        totals = butterfly_sum(
            jnp.stack([jnp.sum(fields[:, 0], dtype=jnp.float32), jnp.sum(advected_sums)]),
            ("gz", "gy", "gx"),
        )
        edge_value = jnp.where(my_layer == 0, solved[..., -1], solved[..., 0])
        other_value = from_partner(edge_value, "gz", 0)
        low_value = jnp.where(my_layer == 0, edge_value, other_value)
        high_value = jnp.where(my_layer == 0, other_value, edge_value)
        lower_end, upper_end = interface_values(low_value, low_spike, high_value, high_spike)
        needed = jnp.where(my_layer == 0, upper_end, lower_end)
        unscaled = solved - spike_column[:, :, None, :] * needed[..., None]
        next_turbulence = unscaled[:, 1].astype(jnp.bfloat16)
        if not last:
            arrived_turbulence = exchange(next_turbulence)
        mass_fixer = totals[0] / totals[1]
        ratios.append(mass_fixer)
        next_concentration = (mass_fixer * unscaled[:, 0]).astype(jnp.bfloat16)
        if not last:
            arrived = jnp.stack([exchange(next_concentration), arrived_turbulence], axis=1)
        fields = jnp.stack([next_concentration, next_turbulence], axis=1)
    return (fields[:, 0], fields[:, 1], jnp.stack(ratios))


def solution(mesh):
    return jax.shard_map(
        per_device,
        mesh=mesh,
        in_specs=(
            P(("gx", "gy"), None, "gz"),
            P(("gx", "gy"), None, "gz"),
            P(("gx", "gy"), None),
            P(("gx", "gy"), None, None, None),
            P(("gx", "gy"), "gz"),
            P(),
            P(),
        ),
        out_specs=(P(("gx", "gy"), None, "gz"), P(("gx", "gy"), None, "gz"), P()),
        check_vma=False,
    )
```

```python
import jax
import jax.numpy as jnp
from jax import lax
from jax.sharding import PartitionSpec as P
from jax.experimental import pallas as pl
from jax.experimental.pallas import tpu as pltpu

STEPS = 2


HIGHEST = lax.Precision.HIGHEST


def passed_along(array, axis, by):
    devices = lax.axis_size(axis)
    pairs = [(i, i + by) for i in range(devices) if 0 <= i + by < devices]
    return lax.ppermute(array, axis, pairs)


def from_partner(array, axis, apart):
    return lax.ppermute(array, axis, [(i, i ^ 1 << apart) for i in range(lax.axis_size(axis))])


def butterfly_sum(value, axes):
    for axis in axes:
        devices = lax.axis_size(axis)
        if devices & (devices - 1):
            value = lax.psum(value, axis)
            continue
        bit = 1
        while bit < devices:
            value = value + lax.ppermute(value, axis, [(i, i ^ bit) for i in range(devices)])
            bit *= 2
    return value


def bucket_ranks(owners, wanted, buckets):
    onehot = (
        (owners[..., None] == jnp.arange(buckets, dtype=jnp.int32)) & wanted[..., None]
    ).astype(jnp.int32)
    running = jnp.cumsum(onehot, axis=-2) - 1
    return jnp.sum(onehot * running, axis=-1)


def table_lookup(level_class, lookup_table):
    classes = lookup_table.shape[-1]
    onehot = (level_class[..., None] == jnp.arange(classes, dtype=jnp.int32)).astype(jnp.float32)
    return jnp.einsum("tzq,fq->tfz", onehot, lookup_table, precision=HIGHEST)


def thomas_inverse_kernel(lower_ref, diagonal_ref, upper_ref, inverse_ref, ratio_ref):
    levels = inverse_ref.shape[0]
    lane = lax.broadcasted_iota(jnp.int32, inverse_ref.shape[1:], 1)
    pivot = 1.0 / diagonal_ref[0]
    ratio = upper_ref[0] * pivot
    row = jnp.where(lane == 0, 1.0, 0.0) * pivot
    ratio_ref[0] = ratio
    inverse_ref[0] = row

    def forward(z, carry):
        ratio, row = carry
        below = lower_ref[z]
        pivot = 1.0 / (diagonal_ref[z] - below * ratio)
        ratio = upper_ref[z] * pivot
        row = (jnp.where(lane == z, 1.0, 0.0) - below * row) * pivot
        ratio_ref[z] = ratio
        inverse_ref[z] = row
        return ratio, row

    _, row = lax.fori_loop(1, levels, forward, (ratio, row), unroll=8)

    def backward(step, row):
        z = levels - 2 - step
        row = inverse_ref[z] - ratio_ref[z] * row
        inverse_ref[z] = row
        return row

    lax.fori_loop(0, levels - 1, backward, row, unroll=8)


def block_inverse(lower, diagonal, upper, ready):
    lead = diagonal.shape[:-1]
    levels = diagonal.shape[-1]
    systems = diagonal.size // levels

    def level_major(band):
        return jnp.broadcast_to(
            jnp.transpose(band.reshape(systems, levels))[:, :, None], (levels, systems, levels)
        )

    bands, ready = lax.optimization_barrier(
        ((level_major(lower), level_major(diagonal), level_major(upper)), ready)
    )
    inverse = pl.pallas_call(
        thomas_inverse_kernel,
        out_shape=jax.ShapeDtypeStruct((levels, systems, levels), jnp.float32),
        scratch_shapes=[pltpu.VMEM((levels, systems, levels), jnp.float32)],
        cost_estimate=pl.CostEstimate(
            flops=16 * levels * systems * levels,
            transcendentals=levels * systems,
            bytes_accessed=64 * levels * systems * levels,
        ),
    )(*bands)
    return jnp.transpose(inverse, (1, 0, 2)).reshape(lead + (levels, levels)), ready


def interface_values(low_value, low_spike, high_value, high_spike):
    lower_end = (low_value - low_spike[..., None] * high_value) / (1.0 - low_spike * high_spike)[
        ..., None
    ]
    upper_end = high_value - high_spike[..., None] * lower_end
    return (lower_end, upper_end)


def per_device(
    concentration, turbulence, src_list, interp_weights, settle_class, kappa_table, fall_table
):
    tiles_here, columns, levels = concentration.shape
    sources_per = src_list.shape[1]
    lane_count = lax.axis_size("gy")
    my_lane = lax.axis_index("gy")
    layers = lax.axis_size("gz")
    my_layer = lax.axis_index("gz")
    remote_count = tiles_here // 2
    capacity = max(2, 3 * remote_count // (2 * (lane_count - 1)))
    lane_rows = src_list.reshape(lane_count, tiles_here * sources_per)
    entries = lax.dynamic_index_in_dim(lane_rows, my_lane, 0, keepdims=False)
    owner_lane = entries // tiles_here % lane_count
    local_tile = entries % tiles_here
    remote = owner_lane != my_lane
    slot_index = bucket_ranks(owner_lane, remote, lane_count)
    reader_owner = lane_rows // tiles_here % lane_count
    reader_tile = lane_rows % tiles_here
    reader_remote = reader_owner != jnp.arange(lane_count, dtype=jnp.int32)[:, None]
    reader_slot = bucket_ranks(reader_owner, reader_remote, lane_count)
    hit = (
        reader_remote[:, None, :]
        & (reader_owner[:, None, :] == my_lane)
        & (reader_slot[:, None, :] == jnp.arange(capacity, dtype=jnp.int32)[None, :, None])
    )
    wanted = jnp.sum(jnp.where(hit, reader_tile[:, None, :], 0), axis=-1, dtype=jnp.int32)
    pool_index = jnp.where(
        remote, tiles_here + owner_lane * capacity + slot_index, local_tile
    ).reshape(tiles_here, sources_per)
    level_class = jnp.repeat(settle_class, levels // settle_class.shape[1], axis=1)
    both_fall = jnp.stack([fall_table, jnp.zeros_like(fall_table)])
    diffusion = table_lookup(level_class, kappa_table)
    falling = table_lookup(level_class, both_fall)
    global_level = my_layer * levels + jnp.arange(levels, dtype=jnp.int32)
    diffusion = jnp.where(global_level >= 1, diffusion, 0.0)
    above_class = passed_along(settle_class[:, :1], "gz", -1)
    at_top = my_layer == layers - 1
    diffusion_above = jnp.where(at_top, 0.0, table_lookup(above_class, kappa_table))
    fall_above = jnp.where(at_top, 0.0, table_lookup(above_class, both_fall))
    diffusion_up = jnp.concatenate([diffusion[..., 1:], diffusion_above], axis=-1)
    fall_up = jnp.concatenate([falling[..., 1:], fall_above], axis=-1)
    diagonal = 1.0 + diffusion + diffusion_up + falling
    lower_band = -diffusion
    upper_band = -(diffusion_up + fall_up)
    level_index = jnp.arange(levels, dtype=jnp.int32)
    block_lower = jnp.where(level_index == 0, 0.0, lower_band)
    block_upper = jnp.where(level_index == levels - 1, 0.0, upper_band)
    fields = jnp.stack([concentration, turbulence], axis=1)

    def exchange(tiles):
        sent = lax.all_to_all(tiles[wanted], "gy", split_axis=0, concat_axis=0, tiled=True)
        return sent.reshape((-1,) + tiles.shape[1:])

    arrived = exchange(fields)
    inverse, wanted = block_inverse(block_lower, diagonal, block_upper, wanted)
    coupled = lax.broadcasted_iota(jnp.int32, (levels,), 0) == jnp.where(
        my_layer == 0, levels - 1, 0
    )
    inverse_column = jnp.sum(jnp.where(coupled, inverse, 0.0), axis=-1)
    spike_column = (
        jnp.where(my_layer == 0, upper_band[..., -1:], lower_band[..., :1]) * inverse_column
    )
    edge_spike = jnp.where(my_layer == 0, spike_column[..., -1], spike_column[..., 0])
    other_spike = from_partner(edge_spike, "gz", 0)
    low_spike = jnp.where(my_layer == 0, edge_spike, other_spike)
    high_spike = jnp.where(my_layer == 0, other_spike, edge_spike)
    ratios = []
    for step_index in range(STEPS):
        tile_pool = jnp.concatenate([fields, arrived], axis=0)
        advected = jnp.zeros(fields.shape, jnp.float32)
        for entry_k in range(sources_per):
            advected = advected + jnp.einsum(
                "tcd,tfdz->tfcz",
                interp_weights[:, entry_k],
                tile_pool[pool_index[:, entry_k]],
                preferred_element_type=jnp.float32,
            )
        last = step_index + 1 == STEPS
        totals = butterfly_sum(
            jnp.stack([jnp.sum(fields[:, 0], dtype=jnp.float32), jnp.sum(advected[:, 0])]),
            ("gz", "gy", "gx"),
        )
        solved = jnp.einsum(
            "tfzy,tfcy->tfcz",
            inverse,
            advected,
            precision=HIGHEST,
            preferred_element_type=jnp.float32,
        )
        edge_value = jnp.where(my_layer == 0, solved[..., -1], solved[..., 0])
        other_value = from_partner(edge_value, "gz", 0)
        low_value = jnp.where(my_layer == 0, edge_value, other_value)
        high_value = jnp.where(my_layer == 0, other_value, edge_value)
        lower_end, upper_end = interface_values(low_value, low_spike, high_value, high_spike)
        needed = jnp.where(my_layer == 0, upper_end, lower_end)
        unscaled = solved - spike_column[:, :, None, :] * needed[..., None]
        next_turbulence = unscaled[:, 1].astype(jnp.bfloat16)
        if not last:
            arrived_turbulence = exchange(next_turbulence)
        mass_fixer = totals[0] / totals[1]
        ratios.append(mass_fixer)
        next_concentration = (mass_fixer * unscaled[:, 0]).astype(jnp.bfloat16)
        if not last:
            arrived = jnp.stack([exchange(next_concentration), arrived_turbulence], axis=1)
        fields = jnp.stack([next_concentration, next_turbulence], axis=1)
    return (fields[:, 0], fields[:, 1], jnp.stack(ratios))


def solution(mesh):
    return jax.shard_map(
        per_device,
        mesh=mesh,
        in_specs=(
            P(("gx", "gy"), None, "gz"),
            P(("gx", "gy"), None, "gz"),
            P("gx", None),
            P(("gx", "gy"), None, None, None),
            P(("gx", "gy"), "gz"),
            P(),
            P(),
        ),
        out_specs=(P(("gx", "gy"), None, "gz"), P(("gx", "gy"), None, "gz"), P()),
        check_vma=False,
    )
```

```python
import jax
import jax.numpy as jnp
from jax import lax
from jax.sharding import PartitionSpec as P
from jax.experimental import pallas as pl
from jax.experimental.pallas import tpu as pltpu

STEPS = 2


HIGHEST = lax.Precision.HIGHEST


def passed_along(array, axis, by):
    devices = lax.axis_size(axis)
    pairs = [(i, i + by) for i in range(devices) if 0 <= i + by < devices]
    return lax.ppermute(array, axis, pairs)


def from_partner(array, axis, apart):
    return lax.ppermute(array, axis, [(i, i ^ 1 << apart) for i in range(lax.axis_size(axis))])


def butterfly_sum(value, axes):
    for axis in axes:
        devices = lax.axis_size(axis)
        if devices & (devices - 1):
            value = lax.psum(value, axis)
            continue
        bit = 1
        while bit < devices:
            value = value + lax.ppermute(value, axis, [(i, i ^ bit) for i in range(devices)])
            bit *= 2
    return value


def bucket_ranks(owners, wanted, buckets):
    onehot = (
        (owners[..., None] == jnp.arange(buckets, dtype=jnp.int32)) & wanted[..., None]
    ).astype(jnp.int32)
    running = jnp.cumsum(onehot, axis=-2) - 1
    return jnp.sum(onehot * running, axis=-1)


def table_lookup(level_class, lookup_table):
    classes = lookup_table.shape[-1]
    onehot = (level_class[..., None] == jnp.arange(classes, dtype=jnp.int32)).astype(jnp.float32)
    return jnp.einsum("tzq,fq->tfz", onehot, lookup_table, precision=HIGHEST)


def thomas_inverse_kernel(lower_ref, diagonal_ref, upper_ref, inverse_ref, ratio_ref):
    levels = inverse_ref.shape[0]
    lane = lax.broadcasted_iota(jnp.int32, inverse_ref.shape[1:], 1)
    pivot = 1.0 / diagonal_ref[0]
    ratio = upper_ref[0] * pivot
    row = jnp.where(lane == 0, 1.0, 0.0) * pivot
    ratio_ref[0] = ratio
    inverse_ref[0] = row

    def forward(z, carry):
        ratio, row = carry
        below = lower_ref[z]
        pivot = 1.0 / (diagonal_ref[z] - below * ratio)
        ratio = upper_ref[z] * pivot
        row = (jnp.where(lane == z, 1.0, 0.0) - below * row) * pivot
        ratio_ref[z] = ratio
        inverse_ref[z] = row
        return ratio, row

    _, row = lax.fori_loop(1, levels, forward, (ratio, row), unroll=8)

    def backward(step, row):
        z = levels - 2 - step
        row = inverse_ref[z] - ratio_ref[z] * row
        inverse_ref[z] = row
        return row

    lax.fori_loop(0, levels - 1, backward, row, unroll=8)


def block_inverse(lower, diagonal, upper, ready):
    lead = diagonal.shape[:-1]
    levels = diagonal.shape[-1]
    systems = diagonal.size // levels

    def level_major(band):
        return jnp.broadcast_to(
            jnp.transpose(band.reshape(systems, levels))[:, :, None], (levels, systems, levels)
        )

    bands, ready = lax.optimization_barrier(
        ((level_major(lower), level_major(diagonal), level_major(upper)), ready)
    )
    inverse = pl.pallas_call(
        thomas_inverse_kernel,
        out_shape=jax.ShapeDtypeStruct((levels, systems, levels), jnp.float32),
        scratch_shapes=[pltpu.VMEM((levels, systems, levels), jnp.float32)],
        cost_estimate=pl.CostEstimate(
            flops=16 * levels * systems * levels,
            transcendentals=levels * systems,
            bytes_accessed=64 * levels * systems * levels,
        ),
    )(*bands)
    return jnp.transpose(inverse, (1, 0, 2)).reshape(lead + (levels, levels)), ready


def interface_values(low_value, low_spike, high_value, high_spike):
    lower_end = (low_value - low_spike[..., None] * high_value) / (1.0 - low_spike * high_spike)[
        ..., None
    ]
    upper_end = high_value - high_spike[..., None] * lower_end
    return (lower_end, upper_end)


def per_device(
    concentration, turbulence, src_list, interp_weights, settle_class, kappa_table, fall_table
):
    tiles_here, columns, levels = concentration.shape
    sources_per = src_list.shape[1]
    lane_count = lax.axis_size("gy")
    my_lane = lax.axis_index("gy")
    layers = lax.axis_size("gz")
    my_layer = lax.axis_index("gz")
    remote_count = tiles_here // 2
    capacity = max(2, 3 * remote_count // (2 * (lane_count - 1)))
    own_rows = src_list.reshape(-1)
    by_hop = [own_rows] + [
        lax.ppermute(own_rows, "gy", [(i, (i + hop) % lane_count) for i in range(lane_count)])
        for hop in range(1, lane_count)
    ]
    lane_rows = jnp.stack(by_hop)[(my_lane - jnp.arange(lane_count)) % lane_count]
    entries = lax.dynamic_index_in_dim(lane_rows, my_lane, 0, keepdims=False)
    owner_lane = entries // tiles_here % lane_count
    local_tile = entries % tiles_here
    remote = owner_lane != my_lane
    slot_index = bucket_ranks(owner_lane, remote, lane_count)
    reader_owner = lane_rows // tiles_here % lane_count
    reader_tile = lane_rows % tiles_here
    reader_remote = reader_owner != jnp.arange(lane_count, dtype=jnp.int32)[:, None]
    reader_slot = bucket_ranks(reader_owner, reader_remote, lane_count)
    hit = (
        reader_remote[:, None, :]
        & (reader_owner[:, None, :] == my_lane)
        & (reader_slot[:, None, :] == jnp.arange(capacity, dtype=jnp.int32)[None, :, None])
    )
    wanted = jnp.sum(jnp.where(hit, reader_tile[:, None, :], 0), axis=-1, dtype=jnp.int32)
    pool_index = jnp.where(
        remote, tiles_here + owner_lane * capacity + slot_index, local_tile
    ).reshape(tiles_here, sources_per)
    level_class = jnp.repeat(settle_class, levels // settle_class.shape[1], axis=1)
    both_fall = jnp.stack([fall_table, jnp.zeros_like(fall_table)])
    diffusion = table_lookup(level_class, kappa_table)
    falling = table_lookup(level_class, both_fall)
    global_level = my_layer * levels + jnp.arange(levels, dtype=jnp.int32)
    diffusion = jnp.where(global_level >= 1, diffusion, 0.0)
    above_class = passed_along(settle_class[:, :1], "gz", -1)
    at_top = my_layer == layers - 1
    diffusion_above = jnp.where(at_top, 0.0, table_lookup(above_class, kappa_table))
    fall_above = jnp.where(at_top, 0.0, table_lookup(above_class, both_fall))
    diffusion_up = jnp.concatenate([diffusion[..., 1:], diffusion_above], axis=-1)
    fall_up = jnp.concatenate([falling[..., 1:], fall_above], axis=-1)
    diagonal = 1.0 + diffusion + diffusion_up + falling
    lower_band = -diffusion
    upper_band = -(diffusion_up + fall_up)
    level_index = jnp.arange(levels, dtype=jnp.int32)
    block_lower = jnp.where(level_index == 0, 0.0, lower_band)
    block_upper = jnp.where(level_index == levels - 1, 0.0, upper_band)
    fields = jnp.stack([concentration, turbulence], axis=1)

    def exchange(tiles):
        sent = lax.all_to_all(tiles[wanted], "gy", split_axis=0, concat_axis=0, tiled=True)
        return sent.reshape((-1,) + tiles.shape[1:])

    arrived = exchange(fields)
    inverse, wanted = block_inverse(block_lower, diagonal, block_upper, wanted)
    coupled = lax.broadcasted_iota(jnp.int32, (levels,), 0) == jnp.where(
        my_layer == 0, levels - 1, 0
    )
    inverse_column = jnp.sum(jnp.where(coupled, inverse, 0.0), axis=-1)
    spike_column = (
        jnp.where(my_layer == 0, upper_band[..., -1:], lower_band[..., :1]) * inverse_column
    )
    edge_spike = jnp.where(my_layer == 0, spike_column[..., -1], spike_column[..., 0])
    other_spike = from_partner(edge_spike, "gz", 0)
    low_spike = jnp.where(my_layer == 0, edge_spike, other_spike)
    high_spike = jnp.where(my_layer == 0, other_spike, edge_spike)
    ratios = []
    for step_index in range(STEPS):
        tile_pool = jnp.concatenate([fields, arrived], axis=0)
        advected = jnp.zeros(fields.shape, jnp.float32)
        for entry_k in range(sources_per):
            advected = advected + jnp.einsum(
                "tcd,tfdz->tfcz",
                interp_weights[:, entry_k],
                tile_pool[pool_index[:, entry_k]],
                preferred_element_type=jnp.float32,
            )
        last = step_index + 1 == STEPS
        totals = butterfly_sum(
            jnp.stack([jnp.sum(fields[:, 0], dtype=jnp.float32), jnp.sum(advected[:, 0])]),
            ("gz", "gy", "gx"),
        )
        solved = jnp.einsum(
            "tfzy,tfcy->tfcz",
            inverse,
            advected,
            precision=HIGHEST,
            preferred_element_type=jnp.float32,
        )
        edge_value = jnp.where(my_layer == 0, solved[..., -1], solved[..., 0])
        other_value = from_partner(edge_value, "gz", 0)
        low_value = jnp.where(my_layer == 0, edge_value, other_value)
        high_value = jnp.where(my_layer == 0, other_value, edge_value)
        lower_end, upper_end = interface_values(low_value, low_spike, high_value, high_spike)
        needed = jnp.where(my_layer == 0, upper_end, lower_end)
        unscaled = solved - spike_column[:, :, None, :] * needed[..., None]
        next_turbulence = unscaled[:, 1].astype(jnp.bfloat16)
        if not last:
            arrived_turbulence = exchange(next_turbulence)
        mass_fixer = totals[0] / totals[1]
        ratios.append(mass_fixer)
        next_concentration = (mass_fixer * unscaled[:, 0]).astype(jnp.bfloat16)
        if not last:
            arrived = jnp.stack([exchange(next_concentration), arrived_turbulence], axis=1)
        fields = jnp.stack([next_concentration, next_turbulence], axis=1)
    return (fields[:, 0], fields[:, 1], jnp.stack(ratios))


def solution(mesh):
    return jax.shard_map(
        per_device,
        mesh=mesh,
        in_specs=(
            P(("gx", "gy"), None, "gz"),
            P(("gx", "gy"), None, "gz"),
            P(("gx", "gy"), None),
            P(("gx", "gy"), None, None, None),
            P(("gx", "gy"), "gz"),
            P(),
            P(),
        ),
        out_specs=(P(("gx", "gy"), None, "gz"), P(("gx", "gy"), None, "gz"), P()),
        check_vma=False,
    )
```

```python
import jax
import jax.numpy as jnp
from jax import lax
from jax.sharding import PartitionSpec as P
from jax.experimental import pallas as pl
from jax.experimental.pallas import tpu as pltpu

STEPS = 2


HIGHEST = lax.Precision.HIGHEST


def passed_along(array, axis, by):
    devices = lax.axis_size(axis)
    pairs = [(i, i + by) for i in range(devices) if 0 <= i + by < devices]
    return lax.ppermute(array, axis, pairs)


def from_partner(array, axis, apart):
    return lax.ppermute(array, axis, [(i, i ^ 1 << apart) for i in range(lax.axis_size(axis))])


def butterfly_sum(value, axes):
    for axis in axes:
        devices = lax.axis_size(axis)
        if devices & (devices - 1):
            value = lax.psum(value, axis)
            continue
        bit = 1
        while bit < devices:
            value = value + lax.ppermute(value, axis, [(i, i ^ bit) for i in range(devices)])
            bit *= 2
    return value


def bucket_ranks(owners, wanted, buckets):
    onehot = (
        (owners[..., None] == jnp.arange(buckets, dtype=jnp.int32)) & wanted[..., None]
    ).astype(jnp.int32)
    running = jnp.cumsum(onehot, axis=-2) - 1
    return jnp.sum(onehot * running, axis=-1)


def table_lookup(level_class, lookup_table):
    classes = lookup_table.shape[-1]
    onehot = (level_class[..., None] == jnp.arange(classes, dtype=jnp.int32)).astype(jnp.float32)
    return jnp.einsum("tzq,fq->tfz", onehot, lookup_table, precision=HIGHEST)


def thomas_inverse_kernel(lower_ref, diagonal_ref, upper_ref, inverse_ref, ratio_ref):
    levels = inverse_ref.shape[0]
    lane = lax.broadcasted_iota(jnp.int32, inverse_ref.shape[1:], 1)
    pivot = 1.0 / diagonal_ref[0]
    ratio = upper_ref[0] * pivot
    row = jnp.where(lane == 0, 1.0, 0.0) * pivot
    ratio_ref[0] = ratio
    inverse_ref[0] = row

    def forward(z, carry):
        ratio, row = carry
        below = lower_ref[z]
        pivot = 1.0 / (diagonal_ref[z] - below * ratio)
        ratio = upper_ref[z] * pivot
        row = (jnp.where(lane == z, 1.0, 0.0) - below * row) * pivot
        ratio_ref[z] = ratio
        inverse_ref[z] = row
        return ratio, row

    _, row = lax.fori_loop(1, levels, forward, (ratio, row), unroll=8)

    def backward(step, row):
        z = levels - 2 - step
        row = inverse_ref[z] - ratio_ref[z] * row
        inverse_ref[z] = row
        return row

    lax.fori_loop(0, levels - 1, backward, row, unroll=8)


def block_inverse(lower, diagonal, upper, ready):
    lead = diagonal.shape[:-1]
    levels = diagonal.shape[-1]
    systems = diagonal.size // levels

    def level_major(band):
        return jnp.broadcast_to(
            jnp.transpose(band.reshape(systems, levels))[:, :, None], (levels, systems, levels)
        )

    bands, ready = lax.optimization_barrier(
        ((level_major(lower), level_major(diagonal), level_major(upper)), ready)
    )
    inverse = pl.pallas_call(
        thomas_inverse_kernel,
        out_shape=jax.ShapeDtypeStruct((levels, systems, levels), jnp.float32),
        scratch_shapes=[pltpu.VMEM((levels, systems, levels), jnp.float32)],
        cost_estimate=pl.CostEstimate(
            flops=16 * levels * systems * levels,
            transcendentals=levels * systems,
            bytes_accessed=64 * levels * systems * levels,
        ),
    )(*bands)
    return jnp.transpose(inverse, (1, 0, 2)).reshape(lead + (levels, levels)), ready


def interface_values(low_value, low_spike, high_value, high_spike):
    lower_end = (low_value - low_spike[..., None] * high_value) / (1.0 - low_spike * high_spike)[
        ..., None
    ]
    upper_end = high_value - high_spike[..., None] * lower_end
    return (lower_end, upper_end)


def per_device(
    concentration, turbulence, src_list, interp_weights, settle_class, kappa_table, fall_table
):
    tiles_here, columns, levels = concentration.shape
    sources_per = src_list.shape[1]
    lane_count = lax.axis_size("gy")
    my_lane = lax.axis_index("gy")
    layers = lax.axis_size("gz")
    my_layer = lax.axis_index("gz")
    remote_count = tiles_here // 2
    capacity = max(2, 3 * remote_count // (2 * (lane_count - 1)))
    lane_rows = src_list.reshape(lane_count, tiles_here * sources_per)
    entries = lax.dynamic_index_in_dim(lane_rows, my_lane, 0, keepdims=False)
    owner_lane = entries // tiles_here % lane_count
    local_tile = entries % tiles_here
    remote = owner_lane != my_lane
    slot_index = bucket_ranks(owner_lane, remote, lane_count)
    reader_owner = lane_rows // tiles_here % lane_count
    reader_tile = lane_rows % tiles_here
    reader_remote = reader_owner != jnp.arange(lane_count, dtype=jnp.int32)[:, None]
    reader_slot = bucket_ranks(reader_owner, reader_remote, lane_count)
    hit = (
        reader_remote[:, None, :]
        & (reader_owner[:, None, :] == my_lane)
        & (reader_slot[:, None, :] == jnp.arange(capacity, dtype=jnp.int32)[None, :, None])
    )
    wanted = jnp.sum(jnp.where(hit, reader_tile[:, None, :], 0), axis=-1, dtype=jnp.int32)
    pool_index = jnp.where(
        remote, tiles_here + owner_lane * capacity + slot_index, local_tile
    ).reshape(tiles_here, sources_per)
    level_class = jnp.repeat(settle_class, levels // settle_class.shape[1], axis=1)
    both_fall = jnp.stack([fall_table, jnp.zeros_like(fall_table)])
    diffusion = table_lookup(level_class, kappa_table)
    falling = table_lookup(level_class, both_fall)
    global_level = my_layer * levels + jnp.arange(levels, dtype=jnp.int32)
    diffusion = jnp.where(global_level >= 1, diffusion, 0.0)
    above_class = passed_along(settle_class[:, :1], "gz", -1)
    at_top = my_layer == layers - 1
    diffusion_above = jnp.where(at_top, 0.0, table_lookup(above_class, kappa_table))
    fall_above = jnp.where(at_top, 0.0, table_lookup(above_class, both_fall))
    diffusion_up = jnp.concatenate([diffusion[..., 1:], diffusion_above], axis=-1)
    fall_up = jnp.concatenate([falling[..., 1:], fall_above], axis=-1)
    diagonal = 1.0 + diffusion + diffusion_up + falling
    lower_band = -diffusion
    upper_band = -(diffusion_up + fall_up)
    level_index = jnp.arange(levels, dtype=jnp.int32)
    block_lower = jnp.where(level_index == 0, 0.0, lower_band)
    block_upper = jnp.where(level_index == levels - 1, 0.0, upper_band)
    fields = jnp.stack([concentration, turbulence], axis=1)

    def exchange(tiles):
        sent = lax.all_to_all(tiles[wanted], "gy", split_axis=0, concat_axis=0, tiled=True)
        return sent.reshape((-1,) + tiles.shape[1:])

    arrived = exchange(fields)
    inverse, wanted = block_inverse(block_lower, diagonal, block_upper, wanted)
    coupled = lax.broadcasted_iota(jnp.int32, (levels,), 0) == jnp.where(
        my_layer == 0, levels - 1, 0
    )
    inverse_column = jnp.sum(jnp.where(coupled, inverse, 0.0), axis=-1)
    spike_column = (
        jnp.where(my_layer == 0, upper_band[..., -1:], lower_band[..., :1]) * inverse_column
    )
    edge_spike = jnp.where(my_layer == 0, spike_column[..., -1], spike_column[..., 0])
    other_spike = from_partner(edge_spike, "gz", 0)
    low_spike = jnp.where(my_layer == 0, edge_spike, other_spike)
    high_spike = jnp.where(my_layer == 0, other_spike, edge_spike)
    ratios = []
    for step_index in range(STEPS):
        tile_pool = jnp.concatenate([fields, arrived], axis=0)
        advected = jnp.zeros(fields.shape, jnp.float32)
        for entry_k in range(sources_per):
            advected = advected + jnp.einsum(
                "tcd,tfdz->tfcz",
                interp_weights[:, entry_k],
                tile_pool[pool_index[:, entry_k]],
                preferred_element_type=jnp.float32,
            )
        last = step_index + 1 == STEPS
        partial = jnp.stack([jnp.sum(fields[:, 0], dtype=jnp.float32), jnp.sum(advected[:, 0])])
        solved = jnp.einsum(
            "tfzy,tfcy->tfcz",
            inverse,
            advected,
            precision=HIGHEST,
            preferred_element_type=jnp.float32,
        )
        edge_value = jnp.where(my_layer == 0, solved[..., -1], solved[..., 0])
        carried = from_partner(jnp.concatenate([edge_value.reshape(-1), partial]), "gz", 0)
        other_value = carried[: edge_value.size].reshape(edge_value.shape)
        totals = butterfly_sum(partial + carried[edge_value.size :], ("gy", "gx"))
        low_value = jnp.where(my_layer == 0, edge_value, other_value)
        high_value = jnp.where(my_layer == 0, other_value, edge_value)
        lower_end, upper_end = interface_values(low_value, low_spike, high_value, high_spike)
        needed = jnp.where(my_layer == 0, upper_end, lower_end)
        unscaled = solved - spike_column[:, :, None, :] * needed[..., None]
        next_turbulence = unscaled[:, 1].astype(jnp.bfloat16)
        if not last:
            arrived_turbulence = exchange(next_turbulence)
        mass_fixer = totals[0] / totals[1]
        ratios.append(mass_fixer)
        next_concentration = (mass_fixer * unscaled[:, 0]).astype(jnp.bfloat16)
        if not last:
            arrived = jnp.stack([exchange(next_concentration), arrived_turbulence], axis=1)
        fields = jnp.stack([next_concentration, next_turbulence], axis=1)
    return (fields[:, 0], fields[:, 1], jnp.stack(ratios))


def solution(mesh):
    return jax.shard_map(
        per_device,
        mesh=mesh,
        in_specs=(
            P(("gx", "gy"), None, "gz"),
            P(("gx", "gy"), None, "gz"),
            P("gx", None),
            P(("gx", "gy"), None, None, None),
            P(("gx", "gy"), "gz"),
            P(),
            P(),
        ),
        out_specs=(P(("gx", "gy"), None, "gz"), P(("gx", "gy"), None, "gz"), P()),
        check_vma=False,
    )
```

```python
import jax
import jax.numpy as jnp
from jax import lax
from jax.sharding import PartitionSpec as P
from jax.experimental import pallas as pl
from jax.experimental.pallas import tpu as pltpu

STEPS = 2


HIGHEST = lax.Precision.HIGHEST


def passed_along(array, axis, by):
    devices = lax.axis_size(axis)
    pairs = [(i, i + by) for i in range(devices) if 0 <= i + by < devices]
    return lax.ppermute(array, axis, pairs)


def from_partner(array, axis, apart):
    return lax.ppermute(array, axis, [(i, i ^ 1 << apart) for i in range(lax.axis_size(axis))])


def butterfly_sum(value, axes):
    for axis in axes:
        devices = lax.axis_size(axis)
        if devices & (devices - 1):
            value = lax.psum(value, axis)
            continue
        bit = 1
        while bit < devices:
            value = value + lax.ppermute(value, axis, [(i, i ^ bit) for i in range(devices)])
            bit *= 2
    return value


def bucket_ranks(owners, wanted, buckets):
    onehot = (
        (owners[..., None] == jnp.arange(buckets, dtype=jnp.int32)) & wanted[..., None]
    ).astype(jnp.int32)
    running = jnp.cumsum(onehot, axis=-2) - 1
    return jnp.sum(onehot * running, axis=-1)


def table_lookup(level_class, lookup_table):
    classes = lookup_table.shape[-1]
    onehot = (level_class[..., None] == jnp.arange(classes, dtype=jnp.int32)).astype(jnp.float32)
    return jnp.einsum("tzq,fq->tfz", onehot, lookup_table, precision=HIGHEST)


def thomas_inverse_kernel(lower_ref, diagonal_ref, upper_ref, inverse_ref, ratio_ref):
    levels = inverse_ref.shape[0]
    lane = lax.broadcasted_iota(jnp.int32, inverse_ref.shape[1:], 1)
    pivot = 1.0 / diagonal_ref[0]
    ratio = upper_ref[0] * pivot
    row = jnp.where(lane == 0, 1.0, 0.0) * pivot
    ratio_ref[0] = ratio
    inverse_ref[0] = row

    def forward(z, carry):
        ratio, row = carry
        below = lower_ref[z]
        pivot = 1.0 / (diagonal_ref[z] - below * ratio)
        ratio = upper_ref[z] * pivot
        row = (jnp.where(lane == z, 1.0, 0.0) - below * row) * pivot
        ratio_ref[z] = ratio
        inverse_ref[z] = row
        return ratio, row

    _, row = lax.fori_loop(1, levels, forward, (ratio, row), unroll=8)

    def backward(step, row):
        z = levels - 2 - step
        row = inverse_ref[z] - ratio_ref[z] * row
        inverse_ref[z] = row
        return row

    lax.fori_loop(0, levels - 1, backward, row, unroll=8)


def block_inverse(lower, diagonal, upper, ready):
    lead = diagonal.shape[:-1]
    levels = diagonal.shape[-1]
    systems = diagonal.size // levels

    def level_major(band):
        return jnp.broadcast_to(
            jnp.transpose(band.reshape(systems, levels))[:, :, None], (levels, systems, levels)
        )

    bands, ready = lax.optimization_barrier(
        ((level_major(lower), level_major(diagonal), level_major(upper)), ready)
    )
    inverse = pl.pallas_call(
        thomas_inverse_kernel,
        out_shape=jax.ShapeDtypeStruct((levels, systems, levels), jnp.float32),
        scratch_shapes=[pltpu.VMEM((levels, systems, levels), jnp.float32)],
        cost_estimate=pl.CostEstimate(
            flops=16 * levels * systems * levels,
            transcendentals=levels * systems,
            bytes_accessed=64 * levels * systems * levels,
        ),
    )(*bands)
    return jnp.transpose(inverse, (1, 0, 2)).reshape(lead + (levels, levels)), ready


def interface_values(low_value, low_spike, high_value, high_spike):
    lower_end = (low_value - low_spike[..., None] * high_value) / (1.0 - low_spike * high_spike)[
        ..., None
    ]
    upper_end = high_value - high_spike[..., None] * lower_end
    return (lower_end, upper_end)


def per_device(
    concentration, turbulence, src_list, interp_weights, settle_class, kappa_table, fall_table
):
    tiles_here, columns, levels = concentration.shape
    sources_per = src_list.shape[1]
    lane_count = lax.axis_size("gy")
    my_lane = lax.axis_index("gy")
    layers = lax.axis_size("gz")
    my_layer = lax.axis_index("gz")
    remote_count = tiles_here // 2
    capacity = max(2, 3 * remote_count // (2 * (lane_count - 1)))
    lane_rows = src_list.reshape(lane_count, tiles_here * sources_per)
    entries = lax.dynamic_index_in_dim(lane_rows, my_lane, 0, keepdims=False)
    owner_lane = entries // tiles_here % lane_count
    local_tile = entries % tiles_here
    remote = owner_lane != my_lane
    slot_index = bucket_ranks(owner_lane, remote, lane_count)
    reader_owner = lane_rows // tiles_here % lane_count
    reader_tile = lane_rows % tiles_here
    reader_remote = reader_owner != jnp.arange(lane_count, dtype=jnp.int32)[:, None]
    reader_slot = bucket_ranks(reader_owner, reader_remote, lane_count)
    hit = (
        reader_remote[:, None, :]
        & (reader_owner[:, None, :] == my_lane)
        & (reader_slot[:, None, :] == jnp.arange(capacity, dtype=jnp.int32)[None, :, None])
    )
    wanted = jnp.sum(jnp.where(hit, reader_tile[:, None, :], 0), axis=-1, dtype=jnp.int32)
    pool_index = jnp.where(
        remote, tiles_here + owner_lane * capacity + slot_index, local_tile
    ).reshape(tiles_here, sources_per)
    level_class = jnp.repeat(settle_class, levels // settle_class.shape[1], axis=1)
    both_fall = jnp.stack([fall_table, jnp.zeros_like(fall_table)])
    diffusion = table_lookup(level_class, kappa_table)
    falling = table_lookup(level_class, both_fall)
    global_level = my_layer * levels + jnp.arange(levels, dtype=jnp.int32)
    diffusion = jnp.where(global_level >= 1, diffusion, 0.0)
    above_class = passed_along(settle_class[:, :1], "gz", -1)
    at_top = my_layer == layers - 1
    diffusion_above = jnp.where(at_top, 0.0, table_lookup(above_class, kappa_table))
    fall_above = jnp.where(at_top, 0.0, table_lookup(above_class, both_fall))
    diffusion_up = jnp.concatenate([diffusion[..., 1:], diffusion_above], axis=-1)
    fall_up = jnp.concatenate([falling[..., 1:], fall_above], axis=-1)
    diagonal = 1.0 + diffusion + diffusion_up + falling
    lower_band = -diffusion
    upper_band = -(diffusion_up + fall_up)
    level_index = jnp.arange(levels, dtype=jnp.int32)
    block_lower = jnp.where(level_index == 0, 0.0, lower_band)
    block_upper = jnp.where(level_index == levels - 1, 0.0, upper_band)
    fields = jnp.stack([concentration, turbulence], axis=1)

    def exchange(tiles):
        sent = lax.all_to_all(tiles[wanted], "gy", split_axis=0, concat_axis=0, tiled=True)
        return sent.reshape((-1,) + tiles.shape[1:])

    arrived = exchange(fields)
    inverse, wanted = block_inverse(block_lower, diagonal, block_upper, wanted)
    coupled = lax.broadcasted_iota(jnp.int32, (levels,), 0) == jnp.where(
        my_layer == 0, levels - 1, 0
    )
    inverse_column = jnp.sum(jnp.where(coupled, inverse, 0.0), axis=-1)
    spike_column = (
        jnp.where(my_layer == 0, upper_band[..., -1:], lower_band[..., :1]) * inverse_column
    )
    edge_spike = jnp.where(my_layer == 0, spike_column[..., -1], spike_column[..., 0])
    other_spike = from_partner(edge_spike, "gz", 0)
    low_spike = jnp.where(my_layer == 0, edge_spike, other_spike)
    high_spike = jnp.where(my_layer == 0, other_spike, edge_spike)
    ratios = []
    for step_index in range(STEPS):
        per_field = []
        for field_id in range(fields.shape[1]):
            tile_pool = jnp.concatenate([fields[:, field_id], arrived[:, field_id]], axis=0)
            field_sum = jnp.zeros(fields[:, field_id].shape, jnp.float32)
            for entry_k in range(sources_per):
                field_sum = field_sum + jnp.einsum(
                    "tcd,tdz->tcz",
                    interp_weights[:, entry_k],
                    tile_pool[pool_index[:, entry_k]],
                    preferred_element_type=jnp.float32,
                )
            per_field.append(field_sum)
        advected = jnp.stack(per_field, axis=1)
        last = step_index + 1 == STEPS
        totals = butterfly_sum(
            jnp.stack([jnp.sum(fields[:, 0], dtype=jnp.float32), jnp.sum(advected[:, 0])]),
            ("gz", "gy", "gx"),
        )
        solved = jnp.einsum(
            "tfzy,tfcy->tfcz",
            inverse,
            advected,
            precision=HIGHEST,
            preferred_element_type=jnp.float32,
        )
        edge_value = jnp.where(my_layer == 0, solved[..., -1], solved[..., 0])
        other_value = from_partner(edge_value, "gz", 0)
        low_value = jnp.where(my_layer == 0, edge_value, other_value)
        high_value = jnp.where(my_layer == 0, other_value, edge_value)
        lower_end, upper_end = interface_values(low_value, low_spike, high_value, high_spike)
        needed = jnp.where(my_layer == 0, upper_end, lower_end)
        unscaled = solved - spike_column[:, :, None, :] * needed[..., None]
        next_turbulence = unscaled[:, 1].astype(jnp.bfloat16)
        if not last:
            arrived_turbulence = exchange(next_turbulence)
        mass_fixer = totals[0] / totals[1]
        ratios.append(mass_fixer)
        next_concentration = (mass_fixer * unscaled[:, 0]).astype(jnp.bfloat16)
        if not last:
            arrived = jnp.stack([exchange(next_concentration), arrived_turbulence], axis=1)
        fields = jnp.stack([next_concentration, next_turbulence], axis=1)
    return (fields[:, 0], fields[:, 1], jnp.stack(ratios))


def solution(mesh):
    return jax.shard_map(
        per_device,
        mesh=mesh,
        in_specs=(
            P(("gx", "gy"), None, "gz"),
            P(("gx", "gy"), None, "gz"),
            P("gx", None),
            P(("gx", "gy"), None, None, None),
            P(("gx", "gy"), "gz"),
            P(),
            P(),
        ),
        out_specs=(P(("gx", "gy"), None, "gz"), P(("gx", "gy"), None, "gz"), P()),
        check_vma=False,
    )
```

```python
import jax
import jax.numpy as jnp
from jax import lax
from jax.sharding import PartitionSpec as P
from jax.experimental import pallas as pl
from jax.experimental.pallas import tpu as pltpu

STEPS = 2


HIGHEST = lax.Precision.HIGHEST


def passed_along(array, axis, by):
    devices = lax.axis_size(axis)
    pairs = [(i, i + by) for i in range(devices) if 0 <= i + by < devices]
    return lax.ppermute(array, axis, pairs)


def from_partner(array, axis, apart):
    return lax.ppermute(array, axis, [(i, i ^ 1 << apart) for i in range(lax.axis_size(axis))])


def butterfly_sum(value, axes):
    for axis in axes:
        devices = lax.axis_size(axis)
        if devices & (devices - 1):
            value = lax.psum(value, axis)
            continue
        bit = 1
        while bit < devices:
            value = value + lax.ppermute(value, axis, [(i, i ^ bit) for i in range(devices)])
            bit *= 2
    return value


def bucket_ranks(owners, wanted, buckets):
    onehot = (
        (owners[..., None] == jnp.arange(buckets, dtype=jnp.int32)) & wanted[..., None]
    ).astype(jnp.int32)
    running = jnp.cumsum(onehot, axis=-2) - 1
    return jnp.sum(onehot * running, axis=-1)


def table_lookup(level_class, lookup_table):
    classes = lookup_table.shape[-1]
    onehot = (level_class[..., None] == jnp.arange(classes, dtype=jnp.int32)).astype(jnp.float32)
    return jnp.einsum("tzq,fq->tfz", onehot, lookup_table, precision=HIGHEST)


def thomas_inverse_kernel(lower_ref, diagonal_ref, upper_ref, inverse_ref, ratio_ref):
    levels = inverse_ref.shape[0]
    lane = lax.broadcasted_iota(jnp.int32, inverse_ref.shape[1:], 1)
    pivot = 1.0 / diagonal_ref[0]
    ratio = upper_ref[0] * pivot
    row = jnp.where(lane == 0, 1.0, 0.0) * pivot
    ratio_ref[0] = ratio
    inverse_ref[0] = row

    def forward(z, carry):
        ratio, row = carry
        below = lower_ref[z]
        pivot = 1.0 / (diagonal_ref[z] - below * ratio)
        ratio = upper_ref[z] * pivot
        row = (jnp.where(lane == z, 1.0, 0.0) - below * row) * pivot
        ratio_ref[z] = ratio
        inverse_ref[z] = row
        return ratio, row

    _, row = lax.fori_loop(1, levels, forward, (ratio, row), unroll=8)

    def backward(step, row):
        z = levels - 2 - step
        row = inverse_ref[z] - ratio_ref[z] * row
        inverse_ref[z] = row
        return row

    lax.fori_loop(0, levels - 1, backward, row, unroll=8)


def block_inverse(lower, diagonal, upper, ready):
    lead = diagonal.shape[:-1]
    levels = diagonal.shape[-1]
    systems = diagonal.size // levels

    def level_major(band):
        return jnp.broadcast_to(
            jnp.transpose(band.reshape(systems, levels))[:, :, None], (levels, systems, levels)
        )

    bands, ready = lax.optimization_barrier(
        ((level_major(lower), level_major(diagonal), level_major(upper)), ready)
    )
    inverse = pl.pallas_call(
        thomas_inverse_kernel,
        out_shape=jax.ShapeDtypeStruct((levels, systems, levels), jnp.float32),
        scratch_shapes=[pltpu.VMEM((levels, systems, levels), jnp.float32)],
        cost_estimate=pl.CostEstimate(
            flops=16 * levels * systems * levels,
            transcendentals=levels * systems,
            bytes_accessed=64 * levels * systems * levels,
        ),
    )(*bands)
    return jnp.transpose(inverse, (1, 0, 2)).reshape(lead + (levels, levels)), ready


def interface_values(low_value, low_spike, high_value, high_spike):
    lower_end = (low_value - low_spike[..., None] * high_value) / (1.0 - low_spike * high_spike)[
        ..., None
    ]
    upper_end = high_value - high_spike[..., None] * lower_end
    return (lower_end, upper_end)


def per_device(
    concentration, turbulence, src_list, interp_weights, settle_class, kappa_table, fall_table
):
    tiles_here, columns, levels = concentration.shape
    sources_per = src_list.shape[1]
    lane_count = lax.axis_size("gy")
    my_lane = lax.axis_index("gy")
    layers = lax.axis_size("gz")
    my_layer = lax.axis_index("gz")
    remote_count = tiles_here // 2
    capacity = max(2, 3 * remote_count // (2 * (lane_count - 1)))
    lane_rows = src_list.reshape(lane_count, tiles_here * sources_per)
    entries = lax.dynamic_index_in_dim(lane_rows, my_lane, 0, keepdims=False)
    owner_lane = entries // tiles_here % lane_count
    local_tile = entries % tiles_here
    remote = owner_lane != my_lane
    slot_index = bucket_ranks(owner_lane, remote, lane_count)
    reader_owner = lane_rows // tiles_here % lane_count
    reader_tile = lane_rows % tiles_here
    reader_remote = reader_owner != jnp.arange(lane_count, dtype=jnp.int32)[:, None]
    reader_slot = bucket_ranks(reader_owner, reader_remote, lane_count)
    hit = (
        reader_remote[:, None, :]
        & (reader_owner[:, None, :] == my_lane)
        & (reader_slot[:, None, :] == jnp.arange(capacity, dtype=jnp.int32)[None, :, None])
    )
    wanted = jnp.sum(jnp.where(hit, reader_tile[:, None, :], 0), axis=-1, dtype=jnp.int32)
    pool_index = jnp.where(
        remote, tiles_here + owner_lane * capacity + slot_index, local_tile
    ).reshape(tiles_here, sources_per)
    level_class = jnp.repeat(settle_class, levels // settle_class.shape[1], axis=1)
    both_fall = jnp.stack([fall_table, jnp.zeros_like(fall_table)])
    diffusion = table_lookup(level_class, kappa_table)
    falling = table_lookup(level_class, both_fall)
    global_level = my_layer * levels + jnp.arange(levels, dtype=jnp.int32)
    diffusion = jnp.where(global_level >= 1, diffusion, 0.0)
    above_class = passed_along(settle_class[:, :1], "gz", -1)
    at_top = my_layer == layers - 1
    diffusion_above = jnp.where(at_top, 0.0, table_lookup(above_class, kappa_table))
    fall_above = jnp.where(at_top, 0.0, table_lookup(above_class, both_fall))
    diffusion_up = jnp.concatenate([diffusion[..., 1:], diffusion_above], axis=-1)
    fall_up = jnp.concatenate([falling[..., 1:], fall_above], axis=-1)
    diagonal = 1.0 + diffusion + diffusion_up + falling
    lower_band = -diffusion
    upper_band = -(diffusion_up + fall_up)
    level_index = jnp.arange(levels, dtype=jnp.int32)
    block_lower = jnp.where(level_index == 0, 0.0, lower_band)
    block_upper = jnp.where(level_index == levels - 1, 0.0, upper_band)
    fields = jnp.stack([concentration, turbulence], axis=1)

    def exchange(tiles):
        sent = lax.all_to_all(tiles[wanted], "gy", split_axis=0, concat_axis=0, tiled=True)
        return sent.reshape((-1,) + tiles.shape[1:])

    arrived = exchange(fields)
    inverse, wanted = block_inverse(block_lower, diagonal, block_upper, wanted)
    coupled = lax.broadcasted_iota(jnp.int32, (levels,), 0) == jnp.where(
        my_layer == 0, levels - 1, 0
    )
    inverse_column = jnp.sum(jnp.where(coupled, inverse, 0.0), axis=-1)
    spike_column = (
        jnp.where(my_layer == 0, upper_band[..., -1:], lower_band[..., :1]) * inverse_column
    )
    edge_spike = jnp.where(my_layer == 0, spike_column[..., -1], spike_column[..., 0])
    other_spike = from_partner(edge_spike, "gz", 0)
    low_spike = jnp.where(my_layer == 0, edge_spike, other_spike)
    high_spike = jnp.where(my_layer == 0, other_spike, edge_spike)
    ratios = []
    for step_index in range(STEPS):
        tile_pool = jnp.concatenate([fields, arrived], axis=0)
        advected = jnp.zeros(fields.shape, jnp.float32)
        for entry_k in range(sources_per):
            advected = advected + jnp.einsum(
                "tcd,tfdz->tfcz",
                interp_weights[:, entry_k],
                tile_pool[pool_index[:, entry_k]],
                preferred_element_type=jnp.float32,
            )
        last = step_index + 1 == STEPS
        totals = butterfly_sum(
            jnp.stack([jnp.sum(fields[:, 0], dtype=jnp.float32), jnp.sum(advected[:, 0])]),
            ("gz", "gy", "gx"),
        )
        solved = jnp.einsum(
            "tfzy,tfcy->tfcz",
            inverse,
            advected,
            precision=HIGHEST,
            preferred_element_type=jnp.float32,
        )
        edge_value = jnp.where(my_layer == 0, solved[..., -1], solved[..., 0])
        other_value = from_partner(edge_value, "gz", 0)
        low_value = jnp.where(my_layer == 0, edge_value, other_value)
        high_value = jnp.where(my_layer == 0, other_value, edge_value)
        lower_end, upper_end = interface_values(low_value, low_spike, high_value, high_spike)
        needed = jnp.where(my_layer == 0, upper_end, lower_end)
        unscaled = solved - spike_column[:, :, None, :] * needed[..., None]
        next_turbulence = unscaled[:, 1].astype(jnp.bfloat16)
        if not last:
            arrived_turbulence = exchange(next_turbulence)
        mass_fixer = totals[0] / totals[1]
        ratios.append(mass_fixer)
        next_concentration = (mass_fixer * unscaled[:, 0]).astype(jnp.bfloat16)
        if not last:
            payload, next_concentration = lax.optimization_barrier(
                (next_concentration[wanted], next_concentration)
            )
            sent = lax.all_to_all(payload, "gy", split_axis=0, concat_axis=0, tiled=True)
            arrived = jnp.stack(
                [sent.reshape((-1,) + next_concentration.shape[1:]), arrived_turbulence], axis=1
            )
        fields = jnp.stack([next_concentration, next_turbulence], axis=1)
    return (fields[:, 0], fields[:, 1], jnp.stack(ratios))


def solution(mesh):
    return jax.shard_map(
        per_device,
        mesh=mesh,
        in_specs=(
            P(("gx", "gy"), None, "gz"),
            P(("gx", "gy"), None, "gz"),
            P("gx", None),
            P(("gx", "gy"), None, None, None),
            P(("gx", "gy"), "gz"),
            P(),
            P(),
        ),
        out_specs=(P(("gx", "gy"), None, "gz"), P(("gx", "gy"), None, "gz"), P()),
        check_vma=False,
    )
```

```python
import jax
import jax.numpy as jnp
from jax import lax
from jax.sharding import PartitionSpec as P
from jax.experimental import pallas as pl
from jax.experimental.pallas import tpu as pltpu

STEPS = 2


HIGHEST = lax.Precision.HIGHEST


def passed_along(array, axis, by):
    devices = lax.axis_size(axis)
    pairs = [(i, i + by) for i in range(devices) if 0 <= i + by < devices]
    return lax.ppermute(array, axis, pairs)


def from_partner(array, axis, apart):
    return lax.ppermute(array, axis, [(i, i ^ 1 << apart) for i in range(lax.axis_size(axis))])


def butterfly_sum(value, axes):
    for axis in axes:
        devices = lax.axis_size(axis)
        if devices & (devices - 1):
            value = lax.psum(value, axis)
            continue
        bit = 1
        while bit < devices:
            value = value + lax.ppermute(value, axis, [(i, i ^ bit) for i in range(devices)])
            bit *= 2
    return value


def bucket_ranks(owners, wanted, buckets):
    onehot = (
        (owners[..., None] == jnp.arange(buckets, dtype=jnp.int32)) & wanted[..., None]
    ).astype(jnp.int32)
    running = jnp.cumsum(onehot, axis=-2) - 1
    return jnp.sum(onehot * running, axis=-1)


def table_lookup(level_class, lookup_table):
    classes = lookup_table.shape[-1]
    onehot = (level_class[..., None] == jnp.arange(classes, dtype=jnp.int32)).astype(jnp.float32)
    return jnp.einsum("tzq,fq->tfz", onehot, lookup_table, precision=HIGHEST)


def thomas_inverse_kernel(lower_ref, diagonal_ref, upper_ref, inverse_ref, ratio_ref):
    levels = inverse_ref.shape[0]
    lane = lax.broadcasted_iota(jnp.int32, inverse_ref.shape[1:], 1)
    pivot = 1.0 / diagonal_ref[0]
    ratio = upper_ref[0] * pivot
    row = jnp.where(lane == 0, 1.0, 0.0) * pivot
    ratio_ref[0] = ratio
    inverse_ref[0] = row

    def forward(z, carry):
        ratio, row = carry
        below = lower_ref[z]
        pivot = 1.0 / (diagonal_ref[z] - below * ratio)
        ratio = upper_ref[z] * pivot
        row = (jnp.where(lane == z, 1.0, 0.0) - below * row) * pivot
        ratio_ref[z] = ratio
        inverse_ref[z] = row
        return ratio, row

    _, row = lax.fori_loop(1, levels, forward, (ratio, row), unroll=8)

    def backward(step, row):
        z = levels - 2 - step
        row = inverse_ref[z] - ratio_ref[z] * row
        inverse_ref[z] = row
        return row

    lax.fori_loop(0, levels - 1, backward, row, unroll=8)


def block_inverse(lower, diagonal, upper, ready):
    lead = diagonal.shape[:-1]
    levels = diagonal.shape[-1]
    systems = diagonal.size // levels

    def level_major(band):
        return jnp.broadcast_to(
            jnp.transpose(band.reshape(systems, levels))[:, :, None], (levels, systems, levels)
        )

    bands, ready = lax.optimization_barrier(
        ((level_major(lower), level_major(diagonal), level_major(upper)), ready)
    )
    inverse = pl.pallas_call(
        thomas_inverse_kernel,
        out_shape=jax.ShapeDtypeStruct((levels, systems, levels), jnp.float32),
        scratch_shapes=[pltpu.VMEM((levels, systems, levels), jnp.float32)],
        cost_estimate=pl.CostEstimate(
            flops=16 * levels * systems * levels,
            transcendentals=levels * systems,
            bytes_accessed=64 * levels * systems * levels,
        ),
    )(*bands)
    return jnp.transpose(inverse, (1, 0, 2)).reshape(lead + (levels, levels)), ready


def interface_values(low_value, low_spike, high_value, high_spike):
    lower_end = (low_value - low_spike[..., None] * high_value) / (1.0 - low_spike * high_spike)[
        ..., None
    ]
    upper_end = high_value - high_spike[..., None] * lower_end
    return (lower_end, upper_end)


def per_device(
    concentration, turbulence, src_list, interp_weights, settle_class, kappa_table, fall_table
):
    tiles_here, columns, levels = concentration.shape
    sources_per = src_list.shape[1]
    lane_count = lax.axis_size("gy")
    my_lane = lax.axis_index("gy")
    layers = lax.axis_size("gz")
    my_layer = lax.axis_index("gz")
    remote_count = tiles_here // 2
    capacity = max(2, 3 * remote_count // (2 * (lane_count - 1)))
    lane_rows = src_list.reshape(lane_count, tiles_here * sources_per)
    entries = lax.dynamic_index_in_dim(lane_rows, my_lane, 0, keepdims=False)
    owner_lane = entries // tiles_here % lane_count
    local_tile = entries % tiles_here
    remote = owner_lane != my_lane
    slot_index = bucket_ranks(owner_lane, remote, lane_count)
    reader_owner = lane_rows // tiles_here % lane_count
    reader_tile = lane_rows % tiles_here
    reader_remote = reader_owner != jnp.arange(lane_count, dtype=jnp.int32)[:, None]
    reader_slot = bucket_ranks(reader_owner, reader_remote, lane_count)
    hit = (
        reader_remote[:, None, :]
        & (reader_owner[:, None, :] == my_lane)
        & (reader_slot[:, None, :] == jnp.arange(capacity, dtype=jnp.int32)[None, :, None])
    )
    wanted = jnp.sum(jnp.where(hit, reader_tile[:, None, :], 0), axis=-1, dtype=jnp.int32)
    pool_index = jnp.where(
        remote, tiles_here + owner_lane * capacity + slot_index, local_tile
    ).reshape(tiles_here, sources_per)
    level_class = jnp.repeat(settle_class, levels // settle_class.shape[1], axis=1)
    both_fall = jnp.stack([fall_table, jnp.zeros_like(fall_table)])
    diffusion = table_lookup(level_class, kappa_table)
    falling = table_lookup(level_class, both_fall)
    global_level = my_layer * levels + jnp.arange(levels, dtype=jnp.int32)
    diffusion = jnp.where(global_level >= 1, diffusion, 0.0)
    above_class = passed_along(settle_class[:, :1], "gz", -1)
    at_top = my_layer == layers - 1
    diffusion_above = jnp.where(at_top, 0.0, table_lookup(above_class, kappa_table))
    fall_above = jnp.where(at_top, 0.0, table_lookup(above_class, both_fall))
    diffusion_up = jnp.concatenate([diffusion[..., 1:], diffusion_above], axis=-1)
    fall_up = jnp.concatenate([falling[..., 1:], fall_above], axis=-1)
    diagonal = 1.0 + diffusion + diffusion_up + falling
    lower_band = -diffusion
    upper_band = -(diffusion_up + fall_up)
    level_index = jnp.arange(levels, dtype=jnp.int32)
    block_lower = jnp.where(level_index == 0, 0.0, lower_band)
    block_upper = jnp.where(level_index == levels - 1, 0.0, upper_band)
    fields = jnp.stack([concentration, turbulence], axis=1)

    def exchange(tiles):
        sent = lax.all_to_all(tiles[wanted], "gy", split_axis=0, concat_axis=0, tiled=True)
        return sent.reshape((-1,) + tiles.shape[1:])

    arrived = exchange(fields)
    inverse, wanted = block_inverse(block_lower, diagonal, block_upper, wanted)
    coupled = lax.broadcasted_iota(jnp.int32, (levels,), 0) == jnp.where(
        my_layer == 0, levels - 1, 0
    )
    inverse_column = jnp.sum(jnp.where(coupled, inverse, 0.0), axis=-1)
    spike_column = (
        jnp.where(my_layer == 0, upper_band[..., -1:], lower_band[..., :1]) * inverse_column
    )
    edge_spike = jnp.where(my_layer == 0, spike_column[..., -1], spike_column[..., 0])
    other_spike = from_partner(edge_spike, "gz", 0)
    low_spike = jnp.where(my_layer == 0, edge_spike, other_spike)
    high_spike = jnp.where(my_layer == 0, other_spike, edge_spike)
    ratios = []
    for step_index in range(STEPS):
        tile_pool = jnp.concatenate([fields, arrived], axis=0)
        advected = jnp.zeros(fields.shape, jnp.float32)
        for entry_k in range(sources_per):
            advected = advected + jnp.einsum(
                "tcd,tfdz->tfcz",
                interp_weights[:, entry_k],
                tile_pool[pool_index[:, entry_k]],
                preferred_element_type=jnp.float32,
            )
        last = step_index + 1 == STEPS
        partial = jnp.stack([jnp.sum(fields[:, 0], dtype=jnp.float32), jnp.sum(advected[:, 0])])
        if last:
            partial = butterfly_sum(partial, ("gz",))
            advected, partial = lax.optimization_barrier((advected, partial))
            totals = butterfly_sum(partial, ("gy", "gx"))
        else:
            totals = butterfly_sum(partial, ("gz", "gy", "gx"))
        solved = jnp.einsum(
            "tfzy,tfcy->tfcz",
            inverse,
            advected,
            precision=HIGHEST,
            preferred_element_type=jnp.float32,
        )
        edge_value = jnp.where(my_layer == 0, solved[..., -1], solved[..., 0])
        other_value = from_partner(edge_value, "gz", 0)
        low_value = jnp.where(my_layer == 0, edge_value, other_value)
        high_value = jnp.where(my_layer == 0, other_value, edge_value)
        lower_end, upper_end = interface_values(low_value, low_spike, high_value, high_spike)
        needed = jnp.where(my_layer == 0, upper_end, lower_end)
        unscaled = solved - spike_column[:, :, None, :] * needed[..., None]
        next_turbulence = unscaled[:, 1].astype(jnp.bfloat16)
        if not last:
            arrived_turbulence = exchange(next_turbulence)
        mass_fixer = totals[0] / totals[1]
        ratios.append(mass_fixer)
        next_concentration = (mass_fixer * unscaled[:, 0]).astype(jnp.bfloat16)
        if not last:
            arrived = jnp.stack([exchange(next_concentration), arrived_turbulence], axis=1)
        fields = jnp.stack([next_concentration, next_turbulence], axis=1)
    return (fields[:, 0], fields[:, 1], jnp.stack(ratios))


def solution(mesh):
    return jax.shard_map(
        per_device,
        mesh=mesh,
        in_specs=(
            P(("gx", "gy"), None, "gz"),
            P(("gx", "gy"), None, "gz"),
            P("gx", None),
            P(("gx", "gy"), None, None, None),
            P(("gx", "gy"), "gz"),
            P(),
            P(),
        ),
        out_specs=(P(("gx", "gy"), None, "gz"), P(("gx", "gy"), None, "gz"), P()),
        check_vma=False,
    )
```
